512 devices in a mesh: dp: 32 (over y, z_lo), band: 16 (over x, z_hi, core).
Axes of the slice: x: 4, y: 8, z: 8 (z_hi: 2, z_lo: 4; z = z_hi * 4 + z_lo), core: 2. Of those that a mesh axis runs over, the one named last changes fastest.
Arguments:
- cell_states: bfloat16 [64, 32, 128, 768], P('dp', 'band'), may hold values from -6 to 6
- head_grads: bfloat16 [64, 32, 128, 384], P('dp', 'band'), may hold values from -6 to 6
- group_ids: int32 [64, 128, 32], P('dp', 'band'), may hold values from 0 to 7, never falling along the last dimension, each value on 1 to 8 neighbouring positions
- proj_weights: bfloat16 [768, 1152], replicated, may hold values from -0.8694895 to 0.8694895
Outputs:
- input_grad: bfloat16 [64, 32, 128, 768], P('dp', 'band')
- weight_grad: float32 [768, 1152], P('band', 'dp')
The draws below stay inside these ranges and needn't reach their ends.
Inputs may be any that keep to these rules, and one draw needn't show every extreme that they name: `group_ids`: group numbers never fall down the rows of a column; a cell sees the header row 0 and the cells of its own group.
All inputs are finite; a program needn't handle non-finite values.
Results may differ from the reference program's by a relative error of at most 0.008.
Values may be sent and summed in bfloat16 or wider, within the bound.
No kernel may reach another device: no remote copies, remote signals or barrier semaphores. Data moves between devices by JAX's collectives and lax.ppermute only.
A program may use at most 64 MiB of HBM per device.

```python
import math
import jax
import jax.numpy as jnp
import numpy as np
from jax import lax

D = 768
HEADS = 6
HD = 64
ROWS = 32
COLS = 128
TABLES = 64
HA = 384


def draw_proj_weights(key, part):
    width = HEADS * HD
    base = jnp.clip(jax.random.normal(key, (D, 3 * width), jnp.float32), -4.0, 4.0) * D ** (-0.5)
    return base.astype(jnp.bfloat16)


def strengthened(drawn, key, source, target, parts, factor):
    def block_of(dim):
        return (jnp.arange(drawn.shape[dim]) // (drawn.shape[dim] // parts)).reshape((-1,) + (1,) * (drawn.ndim - 1 - dim))

    one_side = jax.random.permutation(key, parts)[block_of(target)]
    second = (block_of(target) + parts // 2) % parts
    return jnp.where((block_of(source) == one_side) | (block_of(source) == second), factor * drawn, drawn)


def block_levels(key, shape, shards, smallest, top_value):
    loudness, own = 1.0, jax.random.fold_in(key, 6)
    for axis_at, blocks in shards:
        draws = jnp.exp(jax.random.uniform(jax.random.fold_in(own, axis_at), (blocks,), jnp.float32, smallest / len(shards), top_value / len(shards)))
        loudness = loudness * jnp.repeat(draws, shape[axis_at] // blocks).reshape([-1 if axis == axis_at else 1 for axis in range(len(shape))])
    return loudness


def split_up(amount, total, bound, lean):
    portions = [(1 << 20) // math.isqrt(standing ** lean) + 1 for standing in range(2, amount + 1)]
    spare, counts = total - bound - (amount - 1), [1] * (amount - 1)
    while spare > 0:
        movable = [i for i in range(amount - 1) if counts[i] < bound]
        pool, left = sum([portions[i] for i in movable]), spare
        for i in movable:
            extra = min(bound - counts[i], max(1, left * portions[i] // pool), spare)
            counts[i] = counts[i] + extra
            spare = spare - extra
    return np.array([bound] + counts)


def ragged(own_key, number_of, total, most, skew):
    if number_of == 2:
        one = jax.random.randint(own_key, (), max(1, total - most), min(most, total - 1) + 1)
        return jnp.stack([one, total - one])
    lengths = jnp.asarray(split_up(number_of, total, most, skew), jnp.int32)
    pairs = (number_of - 1) // 2
    source_of, sink = lengths[1:1 + 2 * pairs:2], lengths[2:2 + 2 * pairs:2]
    room = jnp.minimum(source_of - 1, most - sink)
    passed = jax.random.randint(jax.random.fold_in(own_key, 1), (pairs,), 0, 1 << 20) % (room + 1)
    lengths = lengths.at[1:1 + 2 * pairs:2].set(source_of - passed).at[2:2 + 2 * pairs:2].set(sink + passed)
    return lengths[jax.random.permutation(jax.random.fold_in(own_key, 2), number_of)]


def bell_draw(stream_key, shape, spread, bound, cuts=(), kind=jnp.bfloat16):
    drawn = spread * jax.random.normal(stream_key, shape, jnp.float32)
    if cuts:
        drawn = drawn * block_levels(stream_key, shape, cuts, -0.22, 0.18)
    return jnp.clip(drawn, -bound, bound).astype(kind)


def heavy_noise(own_key, shape, deviation, most, cuts, heavy, kind=jnp.bfloat16):
    result = deviation * jax.random.normal(own_key, shape, jnp.float32)
    if cuts:
        result = result * block_levels(own_key, shape, cuts, -0.22, 0.18)
    return jnp.clip(strengthened(result, jax.random.fold_in(own_key, 3), *heavy), -most, most).astype(kind)


def setup_inputs(seed: int = 0) -> dict:
    seeds = jax.random.split(jax.random.key(seed), 5)
    cell_states = heavy_noise(seeds[0], (TABLES, ROWS, COLS, D), 1.0, 6.0, ((0, 32), (1, 16)), (1, 3, 16, 2.0))
    head_grads = bell_draw(seeds[1], (TABLES, ROWS, COLS, HA), 1.0, 6.0, ((0, 32), (1, 16)))
    group_ids = jax.vmap(lambda own: jnp.searchsorted(jnp.cumsum(ragged(own, 8, ROWS, 8, 2)), jnp.arange(ROWS), side="right"))(jax.random.split(seeds[2], TABLES * COLS)).reshape((TABLES, COLS, ROWS)).astype(jnp.int32)
    proj_weights = draw_proj_weights(jax.random.fold_in(seeds[4], 71), 0)
    return dict(cell_states=cell_states, head_grads=head_grads, group_ids=group_ids, proj_weights=proj_weights)


SCALE = 0.125
EPSILON = 1e-06

def normalize(states):
    widened = states.astype(jnp.float32)
    meansq = lax.optimization_barrier(jnp.mean(widened * widened, axis=-1, keepdims=True))
    inverse = lax.rsqrt(meansq + EPSILON)
    scaled = widened * inverse
    return (scaled, inverse, scaled.astype(jnp.bfloat16))

def project(normed, weights):
    width = weights.shape[1] // 3
    flat = normed.reshape(-1, normed.shape[-1])
    mixed = jnp.dot(flat, weights, preferred_element_type=jnp.float32).astype(jnp.bfloat16)
    mixed = mixed.reshape(normed.shape[:-1] + (3 * width,))
    return (mixed[..., :width], mixed[..., width:2 * width], mixed[..., 2 * width:])

def attend_back(query_rows, key_rows, value_rows, grad_rows, groups):
    shape = query_rows.shape
    split = shape[:-1] + (shape[-1] // HD, HD)
    query_five = query_rows.reshape(split).astype(jnp.float32)
    key_five = key_rows.reshape(split).astype(jnp.float32)
    value_five = value_rows.reshape(split).astype(jnp.float32)
    grad_five = grad_rows.reshape(split).astype(jnp.float32)
    scores = jnp.einsum('bichd,bjchd->bchij', query_five, key_five) * SCALE
    header = lax.broadcasted_iota(jnp.int32, (shape[1], shape[1]), 1) == 0
    visible = (groups[:, :, :, None] == groups[:, :, None, :]) | header
    scores = jnp.where(visible[:, :, None], scores, -1e+30)
    peak = lax.optimization_barrier(jnp.max(scores, axis=-1, keepdims=True))
    expsc = jnp.exp(scores - peak)
    probs = expsc / lax.optimization_barrier(jnp.sum(expsc, axis=-1, keepdims=True))
    probs_low = probs.astype(jnp.bfloat16).astype(jnp.float32)
    value_grad = jnp.einsum('bchij,bichd->bjchd', probs_low, grad_five).astype(jnp.bfloat16)
    prob_grad = jnp.einsum('bichd,bjchd->bchij', grad_five, value_five)
    score_grad = probs * (prob_grad - lax.optimization_barrier(jnp.sum(probs * prob_grad, axis=-1, keepdims=True)))
    score_low = (score_grad * SCALE).astype(jnp.bfloat16).astype(jnp.float32)
    query_grad = jnp.einsum('bchij,bjchd->bichd', score_low, key_five).astype(jnp.bfloat16)
    key_grad = jnp.einsum('bchij,bichd->bjchd', score_low, query_five).astype(jnp.bfloat16)
    return (query_grad.reshape(shape), key_grad.reshape(shape), value_grad.reshape(shape))

def finish(scaled, inverse, normed, all_grads, weights):
    flat_norm = normed.reshape(-1, normed.shape[-1])
    flat_grad = all_grads.reshape(-1, all_grads.shape[-1])
    partial_w = jnp.dot(flat_norm.T, flat_grad, preferred_element_type=jnp.float32)
    normed_grad = jnp.dot(flat_grad, weights.T, preferred_element_type=jnp.float32).reshape(scaled.shape)
    coupling = lax.optimization_barrier(jnp.mean(normed_grad * scaled, axis=-1, keepdims=True))
    state_grad = (inverse * (normed_grad - scaled * coupling)).astype(jnp.bfloat16)
    return (partial_w, state_grad)

def reference(cell_states, head_grads, group_ids, proj_weights):

    def one_table(total, pieces):
        states, grads, groups = pieces
        scaled, inverse, normed = normalize(states)
        query_rows, key_rows, value_rows = project(normed, proj_weights)
        query_grad, key_grad, value_grad = attend_back(query_rows[None], key_rows[None], value_rows[None], grads[None], groups[None])
        all_grads = jnp.concatenate((query_grad, key_grad, value_grad), axis=-1)[0]
        partial_w, state_grad = finish(scaled, inverse, normed, all_grads, proj_weights)
        return (total + partial_w, state_grad)
    start = jnp.zeros((D, 3 * HEADS * HD), jnp.float32)
    total, input_grad = lax.scan(one_table, start, (cell_states, head_grads, group_ids))
    return (input_grad, total)
```

```python
import jax
import jax.numpy as jnp
from jax import lax
from jax.sharding import PartitionSpec as P

HD = 64


SCALE = 0.125
EPSILON = 1e-06


def normalize(states):
    widened = states.astype(jnp.float32)
    meansq = jnp.mean(widened * widened, axis=-1, keepdims=True)
    inverse = lax.rsqrt(meansq + EPSILON)
    scaled = widened * inverse
    return (scaled, inverse, scaled.astype(jnp.bfloat16))


def project(normed, weights):
    width = weights.shape[1] // 3
    flat = normed.reshape(-1, normed.shape[-1])
    mixed = jnp.dot(flat, weights, preferred_element_type=jnp.float32).astype(jnp.bfloat16)
    mixed = mixed.reshape(normed.shape[:-1] + (3 * width,))
    return (mixed[..., :width], mixed[..., width : 2 * width], mixed[..., 2 * width :])


def attend_back(query_rows, key_rows, value_rows, grad_rows, groups):
    shape = query_rows.shape
    split = shape[:-1] + (shape[-1] // HD, HD)
    query_five = query_rows.reshape(split)
    key_five = key_rows.reshape(split)
    value_five = value_rows.reshape(split)
    grad_five = grad_rows.reshape(split)
    scores = (
        jnp.einsum("bichd,bjchd->bchij", query_five, key_five, preferred_element_type=jnp.float32)
        * SCALE
    )
    header = lax.broadcasted_iota(jnp.int32, (shape[1], shape[1]), 1) == 0
    visible = (groups[:, :, :, None] == groups[:, :, None, :]) | header
    scores = jnp.where(visible[:, :, None], scores, -1e30)
    peak = jnp.max(scores, axis=-1, keepdims=True)
    expsc = jnp.exp(scores - peak)
    probs = expsc / jnp.sum(expsc, axis=-1, keepdims=True)
    probs_low = probs.astype(jnp.bfloat16)
    value_grad = jnp.einsum(
        "bchij,bichd->bjchd", probs_low, grad_five, preferred_element_type=jnp.float32
    ).astype(jnp.bfloat16)
    prob_grad = jnp.einsum(
        "bichd,bjchd->bchij", grad_five, value_five, preferred_element_type=jnp.float32
    )
    score_grad = probs * (prob_grad - jnp.sum(probs * prob_grad, axis=-1, keepdims=True))
    score_low = (score_grad * SCALE).astype(jnp.bfloat16)
    query_grad = jnp.einsum(
        "bchij,bjchd->bichd", score_low, key_five, preferred_element_type=jnp.float32
    ).astype(jnp.bfloat16)
    key_grad = jnp.einsum(
        "bchij,bichd->bjchd", score_low, query_five, preferred_element_type=jnp.float32
    ).astype(jnp.bfloat16)
    return (query_grad.reshape(shape), key_grad.reshape(shape), value_grad.reshape(shape))


def finish(scaled, inverse, normed, all_grads, weights):
    flat_norm = normed.reshape(-1, normed.shape[-1])
    flat_grad = all_grads.reshape(-1, all_grads.shape[-1])
    partial_w = lax.dot_general(
        flat_norm, flat_grad, (((0,), (0,)), ((), ())), preferred_element_type=jnp.float32
    )
    normed_grad = lax.dot_general(
        flat_grad, weights, (((1,), (1,)), ((), ())), preferred_element_type=jnp.float32
    )
    normed_grad = normed_grad.reshape(scaled.shape)
    coupling = jnp.mean(normed_grad * scaled, axis=-1, keepdims=True)
    state_grad = (inverse * (normed_grad - scaled * coupling)).astype(jnp.bfloat16)
    return (partial_w, state_grad)


def body(cell_states, head_grads, group_ids, proj_weights):
    tables, rows_here, cols, width = cell_states.shape
    heads_width = head_grads.shape[-1]
    both = jnp.concatenate((cell_states, head_grads), axis=-1)
    both_cols = lax.all_to_all(both, "band", split_axis=2, concat_axis=1, tiled=True)
    states_cols = both_cols[..., :width]
    grad_cols = both_cols[..., width:]
    scaled, inverse, normed = normalize(states_cols)
    query_cols, key_cols, value_cols = project(normed, proj_weights)
    query_grad, key_grad, value_grad = attend_back(
        query_cols, key_cols, value_cols, grad_cols, group_ids
    )
    all_grads = jnp.concatenate((query_grad, key_grad, value_grad), axis=-1)
    partial_w, input_cols = finish(scaled, inverse, normed, all_grads, proj_weights)
    input_grad = lax.all_to_all(input_cols, "band", split_axis=1, concat_axis=2, tiled=True)
    n_band = lax.axis_size("band")
    n_dp = lax.axis_size("dp")
    d_in, d_out = partial_w.shape
    blocks = partial_w.reshape(n_band, d_in // n_band, n_dp, d_out // n_dp)
    blocks = blocks.transpose(0, 2, 1, 3).reshape(n_band * n_dp, d_in // n_band, d_out // n_dp)
    weight_grad = lax.psum_scatter(blocks, ("band", "dp"), scatter_dimension=0, tiled=True)
    weight_grad = weight_grad.reshape(d_in // n_band, d_out // n_dp)
    return (input_grad, weight_grad)


def solution(mesh):
    return jax.shard_map(
        body,
        mesh=mesh,
        in_specs=(
            P("dp", "band", None, None),
            P("dp", "band", None, None),
            P("dp", "band", None),
            P(),
        ),
        out_specs=(P("dp", "band", None, None), P("band", "dp")),
        check_vma=False,
    )
```

```python
import jax
import jax.numpy as jnp
from jax import lax
from jax.sharding import PartitionSpec as P

HD = 64


SCALE = 0.125
EPSILON = 1e-06


def normalize(states):
    widened = states.astype(jnp.float32)
    meansq = jnp.mean(widened * widened, axis=-1, keepdims=True)
    inverse = lax.rsqrt(meansq + EPSILON)
    scaled = widened * inverse
    return (scaled, inverse, scaled.astype(jnp.bfloat16))


def project(normed, weights):
    width = weights.shape[1] // 3
    flat = normed.reshape(-1, normed.shape[-1])
    mixed = jnp.dot(flat, weights, preferred_element_type=jnp.float32).astype(jnp.bfloat16)
    mixed = mixed.reshape(normed.shape[:-1] + (3 * width,))
    return (mixed[..., :width], mixed[..., width : 2 * width], mixed[..., 2 * width :])


def attend_back(query_rows, key_rows, value_rows, grad_rows, groups):
    shape = query_rows.shape
    split = shape[:-1] + (shape[-1] // HD, HD)
    query_five = query_rows.reshape(split)
    key_five = key_rows.reshape(split)
    value_five = value_rows.reshape(split)
    grad_five = grad_rows.reshape(split)
    scores = (
        jnp.einsum("bichd,bjchd->bchij", query_five, key_five, preferred_element_type=jnp.float32)
        * SCALE
    )
    header = lax.broadcasted_iota(jnp.int32, (shape[1], shape[1]), 1) == 0
    visible = (groups[:, :, :, None] == groups[:, :, None, :]) | header
    scores = jnp.where(visible[:, :, None], scores, -1e30)
    peak = jnp.max(scores, axis=-1, keepdims=True)
    expsc = jnp.exp(scores - peak)
    probs = expsc / jnp.sum(expsc, axis=-1, keepdims=True)
    probs_low = probs.astype(jnp.bfloat16)
    value_grad = jnp.einsum(
        "bchij,bichd->bjchd", probs_low, grad_five, preferred_element_type=jnp.float32
    ).astype(jnp.bfloat16)
    prob_grad = jnp.einsum(
        "bichd,bjchd->bchij", grad_five, value_five, preferred_element_type=jnp.float32
    )
    score_grad = probs * (prob_grad - jnp.sum(probs * prob_grad, axis=-1, keepdims=True))
    score_low = (score_grad * SCALE).astype(jnp.bfloat16)
    query_grad = jnp.einsum(
        "bchij,bjchd->bichd", score_low, key_five, preferred_element_type=jnp.float32
    ).astype(jnp.bfloat16)
    key_grad = jnp.einsum(
        "bchij,bichd->bjchd", score_low, query_five, preferred_element_type=jnp.float32
    ).astype(jnp.bfloat16)
    return (query_grad.reshape(shape), key_grad.reshape(shape), value_grad.reshape(shape))


def finish(scaled, inverse, normed, all_grads, weights):
    flat_norm = normed.reshape(-1, normed.shape[-1])
    flat_grad = all_grads.reshape(-1, all_grads.shape[-1])
    partial_w = lax.dot_general(
        flat_norm, flat_grad, (((0,), (0,)), ((), ())), preferred_element_type=jnp.float32
    )
    normed_grad = lax.dot_general(
        flat_grad, weights, (((1,), (1,)), ((), ())), preferred_element_type=jnp.float32
    )
    normed_grad = normed_grad.reshape(scaled.shape)
    coupling = jnp.mean(normed_grad * scaled, axis=-1, keepdims=True)
    state_grad = (inverse * (normed_grad - scaled * coupling)).astype(jnp.bfloat16)
    return (partial_w, state_grad)


def exchange(blocks, dim, band, digit, stride, n):
    mine = lax.dynamic_index_in_dim(blocks, digit, axis=dim, keepdims=False)
    total = mine.astype(jnp.float32)
    n_band = lax.axis_size("band")
    for shift in range(1, n):
        part = lax.dynamic_index_in_dim(blocks, (digit + shift) % n, axis=dim, keepdims=False)
        pairs = []
        for source in range(n_band):
            d = (source // stride) % n
            pairs.append((source, source + (((d + shift) % n) - d) * stride))
        total = total + lax.ppermute(part, "band", pairs)
    return total


def reduce_weight_grad(partial_w):
    n_band = lax.axis_size("band")
    n_dp = lax.axis_size("dp")
    d_in, d_out = partial_w.shape
    rows = d_in // n_band
    band = lax.axis_index("band")
    blocks = partial_w.reshape(n_band // 4, 2, 2, rows, d_out)
    blocks = exchange(blocks, 2, band, band % 2, 1, 2)
    blocks = exchange(blocks, 0, band, band // 4, 4, n_band // 4)
    blocks = exchange(blocks, 0, band, (band // 2) % 2, 2, 2)
    cols = d_out // n_dp
    blocks = blocks.reshape(rows, n_dp, cols).transpose(1, 0, 2)
    blocks = lax.all_to_all(blocks, "dp", 0, 0, tiled=True)
    return blocks.sum(axis=0)


def body(cell_states, head_grads, group_ids, proj_weights):
    tables, rows_here, cols, width = cell_states.shape
    heads_width = head_grads.shape[-1]
    both = jnp.concatenate((cell_states, head_grads), axis=-1)
    both_cols = lax.all_to_all(both, "band", split_axis=2, concat_axis=1, tiled=True)
    states_cols = both_cols[..., :width]
    grad_cols = both_cols[..., width:]
    scaled, inverse, normed = normalize(states_cols)
    query_cols, key_cols, value_cols = project(normed, proj_weights)
    query_grad, key_grad, value_grad = attend_back(
        query_cols, key_cols, value_cols, grad_cols, group_ids
    )
    all_grads = jnp.concatenate((query_grad, key_grad, value_grad), axis=-1)
    partial_w, input_cols = finish(scaled, inverse, normed, all_grads, proj_weights)
    input_grad = lax.all_to_all(input_cols, "band", split_axis=1, concat_axis=2, tiled=True)
    weight_grad = reduce_weight_grad(partial_w)
    return (input_grad, weight_grad)


def solution(mesh):
    return jax.shard_map(
        body,
        mesh=mesh,
        in_specs=(
            P("dp", "band", None, None),
            P("dp", "band", None, None),
            P("dp", "band", None),
            P(),
        ),
        out_specs=(P("dp", "band", None, None), P("band", "dp")),
        check_vma=False,
    )
```

```python
import jax
import jax.numpy as jnp
from jax import lax
from jax.sharding import PartitionSpec as P

HD = 64


SCALE = 0.125
EPSILON = 1e-06


def normalize(states):
    widened = states.astype(jnp.float32)
    meansq = jnp.mean(widened * widened, axis=-1, keepdims=True)
    inverse = lax.rsqrt(meansq + EPSILON)
    scaled = widened * inverse
    return (scaled, inverse, scaled.astype(jnp.bfloat16))


def project(normed, weights):
    width = weights.shape[1] // 3
    flat = normed.reshape(-1, normed.shape[-1])
    mixed = jnp.dot(flat, weights, preferred_element_type=jnp.float32).astype(jnp.bfloat16)
    mixed = mixed.reshape(normed.shape[:-1] + (3 * width,))
    return (mixed[..., :width], mixed[..., width : 2 * width], mixed[..., 2 * width :])


def attend_back(query_rows, key_rows, value_rows, grad_rows, groups):
    shape = query_rows.shape
    split = shape[:-1] + (shape[-1] // HD, HD)
    query_five = query_rows.reshape(split)
    key_five = key_rows.reshape(split)
    value_five = value_rows.reshape(split)
    grad_five = grad_rows.reshape(split)
    scores = (
        jnp.einsum("bichd,bjchd->bchij", query_five, key_five, preferred_element_type=jnp.float32)
        * SCALE
    )
    header = lax.broadcasted_iota(jnp.int32, (shape[1], shape[1]), 1) == 0
    visible = (groups[:, :, :, None] == groups[:, :, None, :]) | header
    scores = jnp.where(visible[:, :, None], scores, -1e30)
    peak = jnp.max(scores, axis=-1, keepdims=True)
    expsc = jnp.exp(scores - peak)
    probs = expsc / jnp.sum(expsc, axis=-1, keepdims=True)
    probs_low = probs.astype(jnp.bfloat16)
    value_grad = jnp.einsum(
        "bchij,bichd->bjchd", probs_low, grad_five, preferred_element_type=jnp.float32
    ).astype(jnp.bfloat16)
    prob_grad = jnp.einsum(
        "bichd,bjchd->bchij", grad_five, value_five, preferred_element_type=jnp.float32
    )
    score_grad = probs * (prob_grad - jnp.sum(probs * prob_grad, axis=-1, keepdims=True))
    score_low = (score_grad * SCALE).astype(jnp.bfloat16)
    query_grad = jnp.einsum(
        "bchij,bjchd->bichd", score_low, key_five, preferred_element_type=jnp.float32
    ).astype(jnp.bfloat16)
    key_grad = jnp.einsum(
        "bchij,bichd->bjchd", score_low, query_five, preferred_element_type=jnp.float32
    ).astype(jnp.bfloat16)
    return (query_grad.reshape(shape), key_grad.reshape(shape), value_grad.reshape(shape))


def finish(scaled, inverse, normed, all_grads, weights):
    flat_norm = normed.reshape(-1, normed.shape[-1])
    flat_grad = all_grads.reshape(-1, all_grads.shape[-1])
    partial_w = lax.dot_general(
        flat_norm, flat_grad, (((0,), (0,)), ((), ())), preferred_element_type=jnp.float32
    )
    normed_grad = lax.dot_general(
        flat_grad, weights, (((1,), (1,)), ((), ())), preferred_element_type=jnp.float32
    )
    normed_grad = normed_grad.reshape(scaled.shape)
    coupling = jnp.mean(normed_grad * scaled, axis=-1, keepdims=True)
    state_grad = (inverse * (normed_grad - scaled * coupling)).astype(jnp.bfloat16)
    return (partial_w, state_grad)


def exchange(blocks, dim, band, digit, stride, n):
    mine = lax.dynamic_index_in_dim(blocks, digit, axis=dim, keepdims=False)
    total = mine.astype(jnp.float32)
    n_band = lax.axis_size("band")
    for shift in range(1, n):
        part = lax.dynamic_index_in_dim(blocks, (digit + shift) % n, axis=dim, keepdims=False)
        pairs = []
        for source in range(n_band):
            d = (source // stride) % n
            pairs.append((source, source + (((d + shift) % n) - d) * stride))
        total = total + lax.ppermute(part, "band", pairs)
    return total


def reduce_weight_grad(partial_w):
    n_band = lax.axis_size("band")
    n_dp = lax.axis_size("dp")
    d_in, d_out = partial_w.shape
    rows = d_in // n_band
    band = lax.axis_index("band")
    blocks = partial_w.reshape(n_band // 4, 2, 2, rows, d_out)
    blocks = exchange(blocks, 2, band, band % 2, 1, 2)
    blocks = exchange(blocks, 0, band, band // 4, 4, n_band // 4)
    blocks = exchange(blocks, 0, band, (band // 2) % 2, 2, 2)
    cols = d_out // n_dp
    blocks = blocks.reshape(rows, n_dp, cols).transpose(1, 0, 2)
    blocks = lax.all_to_all(blocks, "dp", 0, 0, tiled=True)
    return blocks.sum(axis=0)


def column_part(both, groups, proj_weights, width):
    both_cols = lax.all_to_all(both, "band", split_axis=2, concat_axis=1, tiled=True)
    states_cols = both_cols[..., :width]
    grad_cols = both_cols[..., width:]
    scaled, inverse, normed = normalize(states_cols)
    query_cols, key_cols, value_cols = project(normed, proj_weights)
    query_grad, key_grad, value_grad = attend_back(
        query_cols, key_cols, value_cols, grad_cols, groups
    )
    all_grads = jnp.concatenate((query_grad, key_grad, value_grad), axis=-1)
    partial_w, input_cols = finish(scaled, inverse, normed, all_grads, proj_weights)
    input_grad = lax.all_to_all(input_cols, "band", split_axis=1, concat_axis=2, tiled=True)
    return partial_w, input_grad


def body(cell_states, head_grads, group_ids, proj_weights):
    tables = cell_states.shape[0]
    width = cell_states.shape[-1]
    both = jnp.concatenate((cell_states, head_grads), axis=-1)
    partial_w = None
    pieces = []
    for t in range(tables):
        part_w, input_part = column_part(
            both[t : t + 1], group_ids[t : t + 1], proj_weights, width
        )
        partial_w = part_w if partial_w is None else partial_w + part_w
        pieces.append(input_part)
    input_grad = jnp.concatenate(pieces, axis=0)
    weight_grad = reduce_weight_grad(partial_w)
    return (input_grad, weight_grad)


def solution(mesh):
    return jax.shard_map(
        body,
        mesh=mesh,
        in_specs=(
            P("dp", "band", None, None),
            P("dp", "band", None, None),
            P("dp", "band", None),
            P(),
        ),
        out_specs=(P("dp", "band", None, None), P("band", "dp")),
        check_vma=False,
    )
```

```python
import jax
import jax.numpy as jnp
from jax import lax
from jax.sharding import PartitionSpec as P

HD = 64


SCALE = 0.125
EPSILON = 1e-06


def normalize(states):
    widened = states.astype(jnp.float32)
    meansq = jnp.mean(widened * widened, axis=-1, keepdims=True)
    inverse = lax.rsqrt(meansq + EPSILON)
    scaled = widened * inverse
    return (scaled, inverse, scaled.astype(jnp.bfloat16))


def project(normed, weights):
    width = weights.shape[1] // 3
    flat = normed.reshape(-1, normed.shape[-1])
    mixed = jnp.dot(flat, weights, preferred_element_type=jnp.float32).astype(jnp.bfloat16)
    mixed = mixed.reshape(normed.shape[:-1] + (3 * width,))
    return (mixed[..., :width], mixed[..., width : 2 * width], mixed[..., 2 * width :])


def attend_back(query, key, value, grads, groups):
    batch, rows, features = query.shape
    heads = features // HD
    own = (
        lax.broadcasted_iota(jnp.int32, (heads, features), 1) // HD
        == lax.broadcasted_iota(jnp.int32, (heads, features), 0)
    )

    def by_head(x):
        return jnp.where(own[None, :, None, :], x[:, None], jnp.zeros((), x.dtype))

    query_heads = by_head(query)
    key_heads = by_head(key)
    grad_heads = by_head(grads)
    scores = (
        jnp.einsum("bhid,bjd->bhij", query_heads, key, preferred_element_type=jnp.float32)
        * SCALE
    )
    header = lax.broadcasted_iota(jnp.int32, (rows, rows), 1) == 0
    visible = (groups[:, :, None] == groups[:, None, :]) | header
    scores = jnp.where(visible[:, None], scores, -1e30)
    peak = jnp.max(scores, axis=-1, keepdims=True)
    expsc = jnp.exp(scores - peak)
    probs = expsc / jnp.sum(expsc, axis=-1, keepdims=True)
    probs_low = probs.astype(jnp.bfloat16)
    value_grad = jnp.einsum(
        "bhij,bhid->bjd", probs_low, grad_heads, preferred_element_type=jnp.float32
    ).astype(jnp.bfloat16)
    prob_grad = jnp.einsum(
        "bhid,bjd->bhij", grad_heads, value, preferred_element_type=jnp.float32
    )
    score_grad = probs * (prob_grad - jnp.sum(probs * prob_grad, axis=-1, keepdims=True))
    score_low = (score_grad * SCALE).astype(jnp.bfloat16)
    query_grad = jnp.einsum(
        "bhij,bhjd->bid", score_low, key_heads, preferred_element_type=jnp.float32
    ).astype(jnp.bfloat16)
    key_grad = jnp.einsum(
        "bhij,bhid->bjd", score_low, query_heads, preferred_element_type=jnp.float32
    ).astype(jnp.bfloat16)
    return (query_grad, key_grad, value_grad)


def finish(scaled, inverse, normed, all_grads, weights):
    flat_norm = normed.reshape(-1, normed.shape[-1])
    flat_grad = all_grads.reshape(-1, all_grads.shape[-1])
    partial_w = lax.dot_general(
        flat_norm, flat_grad, (((0,), (0,)), ((), ())), preferred_element_type=jnp.float32
    )
    normed_grad = lax.dot_general(
        flat_grad, weights, (((1,), (1,)), ((), ())), preferred_element_type=jnp.float32
    )
    normed_grad = normed_grad.reshape(scaled.shape)
    coupling = jnp.mean(normed_grad * scaled, axis=-1, keepdims=True)
    state_grad = (inverse * (normed_grad - scaled * coupling)).astype(jnp.bfloat16)
    return (partial_w, state_grad)


def exchange(blocks, dim, band, digit, stride, n):
    mine = lax.dynamic_index_in_dim(blocks, digit, axis=dim, keepdims=False)
    total = mine.astype(jnp.float32)
    n_band = lax.axis_size("band")
    for shift in range(1, n):
        part = lax.dynamic_index_in_dim(blocks, (digit + shift) % n, axis=dim, keepdims=False)
        pairs = []
        for source in range(n_band):
            d = (source // stride) % n
            pairs.append((source, source + (((d + shift) % n) - d) * stride))
        total = total + lax.ppermute(part, "band", pairs)
    return total


def reduce_weight_grad(partial_w):
    n_band = lax.axis_size("band")
    n_dp = lax.axis_size("dp")
    d_in, d_out = partial_w.shape
    rows = d_in // n_band
    band = lax.axis_index("band")
    blocks = partial_w.reshape(n_band // 4, 2, 2, rows, d_out)
    blocks = exchange(blocks, 2, band, band % 2, 1, 2)
    blocks = exchange(blocks, 0, band, band // 4, 4, n_band // 4)
    blocks = exchange(blocks, 0, band, (band // 2) % 2, 2, 2)
    cols = d_out // n_dp
    blocks = blocks.reshape(rows, n_dp, cols).transpose(1, 0, 2)
    blocks = lax.all_to_all(blocks, "dp", 0, 0, tiled=True)
    return blocks.sum(axis=0)


def body(cell_states, head_grads, group_ids, proj_weights):
    width = cell_states.shape[-1]
    both = jnp.concatenate((cell_states, head_grads), axis=-1)
    both_cols = lax.all_to_all(both, "band", split_axis=2, concat_axis=1, tiled=True)
    tables, rows, cols, features = both_cols.shape
    both_cols = both_cols.transpose(0, 2, 1, 3).reshape(tables * cols, rows, features)
    groups = group_ids.reshape(tables * cols, rows)
    states_cols = both_cols[..., :width]
    grad_cols = both_cols[..., width:]
    scaled, inverse, normed = normalize(states_cols)
    query_cols, key_cols, value_cols = project(normed, proj_weights)
    query_grad, key_grad, value_grad = attend_back(
        query_cols, key_cols, value_cols, grad_cols, groups
    )
    all_grads = jnp.concatenate((query_grad, key_grad, value_grad), axis=-1)
    partial_w, input_cols = finish(scaled, inverse, normed, all_grads, proj_weights)
    input_cols = input_cols.reshape(tables, cols, rows, width).transpose(0, 2, 1, 3)
    input_grad = lax.all_to_all(input_cols, "band", split_axis=1, concat_axis=2, tiled=True)
    weight_grad = reduce_weight_grad(partial_w)
    return (input_grad, weight_grad)


def solution(mesh):
    return jax.shard_map(
        body,
        mesh=mesh,
        in_specs=(
            P("dp", "band", None, None),
            P("dp", "band", None, None),
            P("dp", "band", None),
            P(),
        ),
        out_specs=(P("dp", "band", None, None), P("band", "dp")),
        check_vma=False,
    )
```

```python
import jax
import jax.numpy as jnp
from jax import lax
from jax.sharding import PartitionSpec as P

HD = 64


SCALE = 0.125
EPSILON = 1e-06


def normalize(states):
    widened = states.astype(jnp.float32)
    meansq = jnp.mean(widened * widened, axis=-1, keepdims=True)
    inverse = lax.rsqrt(meansq + EPSILON)
    scaled = widened * inverse
    return (scaled, inverse, scaled.astype(jnp.bfloat16))


def project(normed, weights):
    width = weights.shape[1] // 3
    flat = normed.reshape(-1, normed.shape[-1])
    mixed = jnp.dot(flat, weights, preferred_element_type=jnp.float32).astype(jnp.bfloat16)
    mixed = mixed.reshape(normed.shape[:-1] + (3 * width,))
    return (mixed[..., :width], mixed[..., width : 2 * width], mixed[..., 2 * width :])


def attend_back(query, key, value, grads, groups):
    batch, rows, features = query.shape
    heads = features // HD
    own = (
        lax.broadcasted_iota(jnp.int32, (heads, features), 1) // HD
        == lax.broadcasted_iota(jnp.int32, (heads, features), 0)
    )

    def by_head(x):
        return jnp.where(own[None, :, None, :], x[:, None], jnp.zeros((), x.dtype))

    query_heads = by_head(query)
    key_heads = by_head(key)
    grad_heads = by_head(grads)
    scores = (
        jnp.einsum("bhid,bjd->bhij", query_heads, key, preferred_element_type=jnp.float32)
        * SCALE
    )
    header = lax.broadcasted_iota(jnp.int32, (rows, rows), 1) == 0
    visible = (groups[:, :, None] == groups[:, None, :]) | header
    scores = jnp.where(visible[:, None], scores, -1e30)
    peak = jnp.max(scores, axis=-1, keepdims=True)
    expsc = jnp.exp(scores - peak)
    probs = expsc / jnp.sum(expsc, axis=-1, keepdims=True)
    probs_low = probs.astype(jnp.bfloat16)
    value_grad = jnp.einsum(
        "bhij,bhid->bjd", probs_low, grad_heads, preferred_element_type=jnp.float32
    ).astype(jnp.bfloat16)
    prob_grad = jnp.einsum(
        "bhid,bjd->bhij", grad_heads, value, preferred_element_type=jnp.float32
    )
    score_grad = probs * (prob_grad - jnp.sum(probs * prob_grad, axis=-1, keepdims=True))
    score_low = (score_grad * SCALE).astype(jnp.bfloat16)
    query_grad = jnp.einsum(
        "bhij,bhjd->bid", score_low, key_heads, preferred_element_type=jnp.float32
    ).astype(jnp.bfloat16)
    key_grad = jnp.einsum(
        "bhij,bhid->bjd", score_low, query_heads, preferred_element_type=jnp.float32
    ).astype(jnp.bfloat16)
    return (query_grad, key_grad, value_grad)


def finish(scaled, inverse, normed, all_grads, weights):
    flat_norm = normed.reshape(-1, normed.shape[-1])
    flat_grad = all_grads.reshape(-1, all_grads.shape[-1])
    partial_w = lax.dot_general(
        flat_norm, flat_grad, (((0,), (0,)), ((), ())), preferred_element_type=jnp.float32
    )
    normed_grad = lax.dot_general(
        flat_grad, weights, (((1,), (1,)), ((), ())), preferred_element_type=jnp.float32
    )
    normed_grad = normed_grad.reshape(scaled.shape)
    coupling = jnp.mean(normed_grad * scaled, axis=-1, keepdims=True)
    state_grad = (inverse * (normed_grad - scaled * coupling)).astype(jnp.bfloat16)
    return (partial_w, state_grad)


def exchange(blocks, dim, band, digit, stride, n):
    mine = lax.dynamic_index_in_dim(blocks, digit, axis=dim, keepdims=False)
    total = mine.astype(jnp.float32)
    n_band = lax.axis_size("band")
    for shift in range(1, n):
        part = lax.dynamic_index_in_dim(blocks, (digit + shift) % n, axis=dim, keepdims=False)
        pairs = []
        for source in range(n_band):
            d = (source // stride) % n
            pairs.append((source, source + (((d + shift) % n) - d) * stride))
        total = total + lax.ppermute(part, "band", pairs)
    return total


def reduce_weight_grad(partial_w):
    n_band = lax.axis_size("band")
    n_dp = lax.axis_size("dp")
    d_in, d_out = partial_w.shape
    rows = d_in // n_band
    band = lax.axis_index("band")
    blocks = partial_w.reshape(n_band // 4, 2, 2, rows, d_out)
    blocks = exchange(blocks, 2, band, band % 2, 1, 2)
    blocks = exchange(blocks, 0, band, band // 4, 4, n_band // 4)
    blocks = exchange(blocks, 0, band, (band // 2) % 2, 2, 2)
    cols = d_out // n_dp
    blocks = blocks.reshape(rows, n_dp, cols).transpose(1, 0, 2)
    blocks = lax.all_to_all(blocks, "dp", 0, 0, tiled=True)
    return blocks.sum(axis=0)


def body(cell_states, head_grads, group_ids, proj_weights):
    width = cell_states.shape[-1]
    states_cols = lax.all_to_all(cell_states, "band", split_axis=2, concat_axis=1, tiled=True)
    tables, rows, cols, _ = states_cols.shape
    states_cols = states_cols.transpose(0, 2, 1, 3).reshape(tables * cols, rows, width)
    states_cols, head_grads = lax.optimization_barrier((states_cols, head_grads))
    grad_cols = lax.all_to_all(head_grads, "band", split_axis=2, concat_axis=1, tiled=True)
    grad_cols = grad_cols.transpose(0, 2, 1, 3).reshape(tables * cols, rows, -1)
    groups = group_ids.reshape(tables * cols, rows)
    scaled, inverse, normed = normalize(states_cols)
    query_cols, key_cols, value_cols = project(normed, proj_weights)
    query_grad, key_grad, value_grad = attend_back(
        query_cols, key_cols, value_cols, grad_cols, groups
    )
    all_grads = jnp.concatenate((query_grad, key_grad, value_grad), axis=-1)
    partial_w, input_cols = finish(scaled, inverse, normed, all_grads, proj_weights)
    input_cols = input_cols.reshape(tables, cols, rows, width).transpose(0, 2, 1, 3)
    input_grad = lax.all_to_all(input_cols, "band", split_axis=1, concat_axis=2, tiled=True)
    weight_grad = reduce_weight_grad(partial_w)
    return (input_grad, weight_grad)


def solution(mesh):
    return jax.shard_map(
        body,
        mesh=mesh,
        in_specs=(
            P("dp", "band", None, None),
            P("dp", "band", None, None),
            P("dp", "band", None),
            P(),
        ),
        out_specs=(P("dp", "band", None, None), P("band", "dp")),
        check_vma=False,
    )
```

```python
import jax
import jax.numpy as jnp
from jax import lax
from jax.sharding import PartitionSpec as P

HD = 64


SCALE = 0.125
EPSILON = 1e-06


def normalize(states):
    widened = states.astype(jnp.float32)
    meansq = jnp.mean(widened * widened, axis=-1, keepdims=True)
    inverse = lax.rsqrt(meansq + EPSILON)
    scaled = widened * inverse
    return (scaled, inverse, scaled.astype(jnp.bfloat16))


def project(normed, weights):
    width = weights.shape[1] // 3
    flat = normed.reshape(-1, normed.shape[-1])
    mixed = jnp.dot(flat, weights, preferred_element_type=jnp.float32).astype(jnp.bfloat16)
    mixed = mixed.reshape(normed.shape[:-1] + (3 * width,))
    return (mixed[..., :width], mixed[..., width : 2 * width], mixed[..., 2 * width :])


def attend_back(query, key, value, grads, groups):
    batch, rows, features = query.shape
    heads = features // HD
    own = (
        lax.broadcasted_iota(jnp.int32, (heads, features), 1) // HD
        == lax.broadcasted_iota(jnp.int32, (heads, features), 0)
    )

    def by_head(x):
        return jnp.where(own[None, :, None, :], x[:, None], jnp.zeros((), x.dtype))

    query_heads = by_head(query)
    key_heads = by_head(key)
    grad_heads = by_head(grads)
    scores = (
        jnp.einsum("bhid,bjd->bhij", query_heads, key, preferred_element_type=jnp.float32)
        * SCALE
    )
    header = lax.broadcasted_iota(jnp.int32, (rows, rows), 1) == 0
    visible = (groups[:, :, None] == groups[:, None, :]) | header
    scores = jnp.where(visible[:, None], scores, -1e30)
    peak = jnp.max(scores, axis=-1, keepdims=True)
    expsc = jnp.exp(scores - peak)
    probs = expsc / jnp.sum(expsc, axis=-1, keepdims=True)
    probs_low = probs.astype(jnp.bfloat16)
    value_grad = jnp.einsum(
        "bhij,bhid->bjd", probs_low, grad_heads, preferred_element_type=jnp.float32
    ).astype(jnp.bfloat16)
    prob_grad = jnp.einsum(
        "bhid,bjd->bhij", grad_heads, value, preferred_element_type=jnp.float32
    )
    score_grad = probs * (prob_grad - jnp.sum(probs * prob_grad, axis=-1, keepdims=True))
    score_low = (score_grad * SCALE).astype(jnp.bfloat16)
    query_grad = jnp.einsum(
        "bhij,bhjd->bid", score_low, key_heads, preferred_element_type=jnp.float32
    ).astype(jnp.bfloat16)
    key_grad = jnp.einsum(
        "bhij,bhid->bjd", score_low, query_heads, preferred_element_type=jnp.float32
    ).astype(jnp.bfloat16)
    return (query_grad, key_grad, value_grad)


def finish(scaled, inverse, normed, all_grads, weights):
    flat_norm = normed.reshape(-1, normed.shape[-1])
    flat_grad = all_grads.reshape(-1, all_grads.shape[-1])
    partial_w = lax.dot_general(
        flat_norm, flat_grad, (((0,), (0,)), ((), ())), preferred_element_type=jnp.float32
    )
    normed_grad = lax.dot_general(
        flat_grad, weights, (((1,), (1,)), ((), ())), preferred_element_type=jnp.float32
    )
    normed_grad = normed_grad.reshape(scaled.shape)
    coupling = jnp.mean(normed_grad * scaled, axis=-1, keepdims=True)
    state_grad = (inverse * (normed_grad - scaled * coupling)).astype(jnp.bfloat16)
    return (partial_w, state_grad)


def exchange(blocks, dim, band, digit, stride, n):
    mine = lax.dynamic_index_in_dim(blocks, digit, axis=dim, keepdims=False)
    total = mine.astype(jnp.float32)
    n_band = lax.axis_size("band")
    for shift in range(1, n):
        part = lax.dynamic_index_in_dim(blocks, (digit + shift) % n, axis=dim, keepdims=False)
        pairs = []
        for source in range(n_band):
            d = (source // stride) % n
            pairs.append((source, source + (((d + shift) % n) - d) * stride))
        got = lax.ppermute(part.astype(jnp.bfloat16), "band", pairs)
        total = total + got.astype(jnp.float32)
    return total


def reduce_weight_grad(partial_w):
    n_band = lax.axis_size("band")
    n_dp = lax.axis_size("dp")
    d_in, d_out = partial_w.shape
    rows = d_in // n_band
    band = lax.axis_index("band")
    blocks = partial_w.reshape(n_band // 4, 2, 2, rows, d_out)
    blocks = exchange(blocks, 2, band, band % 2, 1, 2)
    blocks = exchange(blocks, 0, band, band // 4, 4, n_band // 4)
    blocks = exchange(blocks, 0, band, (band // 2) % 2, 2, 2)
    cols = d_out // n_dp
    blocks = blocks.reshape(rows, n_dp, cols).transpose(1, 0, 2)
    blocks = lax.all_to_all(blocks.astype(jnp.bfloat16), "dp", 0, 0, tiled=True)
    return blocks.astype(jnp.float32).sum(axis=0)


def body(cell_states, head_grads, group_ids, proj_weights):
    width = cell_states.shape[-1]
    states_cols = lax.all_to_all(cell_states, "band", split_axis=2, concat_axis=1, tiled=True)
    tables, rows, cols, _ = states_cols.shape
    states_cols = states_cols.transpose(0, 2, 1, 3).reshape(tables * cols, rows, width)
    states_cols, head_grads = lax.optimization_barrier((states_cols, head_grads))
    grad_cols = lax.all_to_all(head_grads, "band", split_axis=2, concat_axis=1, tiled=True)
    grad_cols = grad_cols.transpose(0, 2, 1, 3).reshape(tables * cols, rows, -1)
    groups = group_ids.reshape(tables * cols, rows)
    scaled, inverse, normed = normalize(states_cols)
    query_cols, key_cols, value_cols = project(normed, proj_weights)
    query_grad, key_grad, value_grad = attend_back(
        query_cols, key_cols, value_cols, grad_cols, groups
    )
    all_grads = jnp.concatenate((query_grad, key_grad, value_grad), axis=-1)
    partial_w, input_cols = finish(scaled, inverse, normed, all_grads, proj_weights)
    input_cols = input_cols.reshape(tables, cols, rows, width).transpose(0, 2, 1, 3)
    input_grad = lax.all_to_all(input_cols, "band", split_axis=1, concat_axis=2, tiled=True)
    weight_grad = reduce_weight_grad(partial_w)
    return (input_grad, weight_grad)


def solution(mesh):
    return jax.shard_map(
        body,
        mesh=mesh,
        in_specs=(
            P("dp", "band", None, None),
            P("dp", "band", None, None),
            P("dp", "band", None),
            P(),
        ),
        out_specs=(P("dp", "band", None, None), P("band", "dp")),
        check_vma=False,
    )
```

```python
import jax
import jax.numpy as jnp
from jax import lax
from jax.sharding import PartitionSpec as P

HD = 64


SCALE = 0.125
EPSILON = 1e-06


def normalize(states):
    widened = states.astype(jnp.float32)
    meansq = jnp.mean(widened * widened, axis=-1, keepdims=True)
    inverse = lax.rsqrt(meansq + EPSILON)
    scaled = widened * inverse
    return (scaled, inverse, scaled.astype(jnp.bfloat16))


def project(normed, weights):
    width = weights.shape[1] // 3
    flat = normed.reshape(-1, normed.shape[-1])
    mixed = jnp.dot(flat, weights, preferred_element_type=jnp.float32).astype(jnp.bfloat16)
    mixed = mixed.reshape(normed.shape[:-1] + (3 * width,))
    return (mixed[..., :width], mixed[..., width : 2 * width], mixed[..., 2 * width :])


def attend_back(query, key, value, grads, groups):
    batch, rows, features = query.shape
    heads = features // HD
    own = (
        lax.broadcasted_iota(jnp.int32, (heads, features), 1) // HD
        == lax.broadcasted_iota(jnp.int32, (heads, features), 0)
    )

    def by_head(x):
        return jnp.where(own[None, :, None, :], x[:, None], jnp.zeros((), x.dtype))

    query_heads = by_head(query)
    key_heads = by_head(key)
    grad_heads = by_head(grads)
    scores = (
        jnp.einsum("bhid,bjd->bhij", query_heads, key, preferred_element_type=jnp.float32)
        * SCALE
    )
    header = lax.broadcasted_iota(jnp.int32, (rows, rows), 1) == 0
    visible = (groups[:, :, None] == groups[:, None, :]) | header
    scores = jnp.where(visible[:, None], scores, -1e30)
    peak = jnp.max(scores, axis=-1, keepdims=True)
    expsc = jnp.exp(scores - peak)
    probs = expsc / jnp.sum(expsc, axis=-1, keepdims=True)
    probs_low = probs.astype(jnp.bfloat16)
    value_grad = jnp.einsum(
        "bhij,bhid->bjd", probs_low, grad_heads, preferred_element_type=jnp.float32
    ).astype(jnp.bfloat16)
    prob_grad = jnp.einsum(
        "bhid,bjd->bhij", grad_heads, value, preferred_element_type=jnp.float32
    )
    score_grad = probs * (prob_grad - jnp.sum(probs * prob_grad, axis=-1, keepdims=True))
    score_low = (score_grad * SCALE).astype(jnp.bfloat16)
    query_grad = jnp.einsum(
        "bhij,bhjd->bid", score_low, key_heads, preferred_element_type=jnp.float32
    ).astype(jnp.bfloat16)
    key_grad = jnp.einsum(
        "bhij,bhid->bjd", score_low, query_heads, preferred_element_type=jnp.float32
    ).astype(jnp.bfloat16)
    return (query_grad, key_grad, value_grad)


def finish(scaled, inverse, normed, all_grads, weights):
    flat_norm = normed.reshape(-1, normed.shape[-1])
    flat_grad = all_grads.reshape(-1, all_grads.shape[-1])
    partial_w = lax.dot_general(
        flat_norm, flat_grad, (((0,), (0,)), ((), ())), preferred_element_type=jnp.float32
    )
    normed_grad = lax.dot_general(
        flat_grad, weights, (((1,), (1,)), ((), ())), preferred_element_type=jnp.float32
    )
    normed_grad = normed_grad.reshape(scaled.shape)
    coupling = jnp.mean(normed_grad * scaled, axis=-1, keepdims=True)
    state_grad = (inverse * (normed_grad - scaled * coupling)).astype(jnp.bfloat16)
    return (partial_w, state_grad)


def exchange(blocks, dim, digit, stride, n, wire=jnp.float32):
    mine = lax.dynamic_index_in_dim(blocks, digit, axis=dim, keepdims=False)
    total = mine.astype(jnp.float32)
    n_band = lax.axis_size("band")
    for shift in range(1, n):
        part = lax.dynamic_index_in_dim(blocks, (digit + shift) % n, axis=dim, keepdims=False)
        pairs = []
        for source in range(n_band):
            d = (source // stride) % n
            pairs.append((source, source + (((d + shift) % n) - d) * stride))
        got = lax.ppermute(part.astype(wire), "band", pairs)
        total = total + got.astype(jnp.float32)
    return total


def band_stages(partial_w):
    n_band = lax.axis_size("band")
    d_in, d_out = partial_w.shape
    rows = d_in // n_band
    band = lax.axis_index("band")
    blocks = partial_w.reshape(n_band // 4, 2, 2, rows, d_out)
    blocks = exchange(blocks, 2, band % 2, 1, 2)
    blocks = exchange(blocks, 0, band // 4, 4, n_band // 4, jnp.bfloat16)
    return exchange(blocks, 0, (band // 2) % 2, 2, 2)


def dp_stage(blocks):
    n_dp = lax.axis_size("dp")
    rows, d_out = blocks.shape
    cols = d_out // n_dp
    blocks = blocks.reshape(rows, n_dp, cols).transpose(1, 0, 2)
    blocks = lax.all_to_all(blocks, "dp", 0, 0, tiled=True)
    return blocks.sum(axis=0)


def body(cell_states, head_grads, group_ids, proj_weights):
    width = cell_states.shape[-1]
    states_cols = lax.all_to_all(cell_states, "band", split_axis=2, concat_axis=1, tiled=True)
    tables, rows, cols, _ = states_cols.shape
    states_cols = states_cols.transpose(0, 2, 1, 3).reshape(tables * cols, rows, width)
    states_cols, head_grads = lax.optimization_barrier((states_cols, head_grads))
    grad_cols = lax.all_to_all(head_grads, "band", split_axis=2, concat_axis=1, tiled=True)
    grad_cols = grad_cols.transpose(0, 2, 1, 3).reshape(tables * cols, rows, -1)
    groups = group_ids.reshape(tables * cols, rows)
    scaled, inverse, normed = normalize(states_cols)
    query_cols, key_cols, value_cols = project(normed, proj_weights)
    query_grad, key_grad, value_grad = attend_back(
        query_cols, key_cols, value_cols, grad_cols, groups
    )
    all_grads = jnp.concatenate((query_grad, key_grad, value_grad), axis=-1)
    partial_w, input_cols = finish(scaled, inverse, normed, all_grads, proj_weights)
    input_cols = input_cols.reshape(tables, cols, rows, width).transpose(0, 2, 1, 3)
    input_cols, partial_w = lax.optimization_barrier((input_cols, partial_w))
    input_grad = lax.all_to_all(input_cols, "band", split_axis=1, concat_axis=2, tiled=True)
    reduced = band_stages(partial_w)
    reduced, input_grad = lax.optimization_barrier((reduced, input_grad))
    weight_grad = dp_stage(reduced)
    return (input_grad, weight_grad)


def solution(mesh):
    return jax.shard_map(
        body,
        mesh=mesh,
        in_specs=(
            P("dp", "band", None, None),
            P("dp", "band", None, None),
            P("dp", "band", None),
            P(),
        ),
        out_specs=(P("dp", "band", None, None), P("band", "dp")),
        check_vma=False,
    )
```

```python
import jax
import jax.numpy as jnp
from jax import lax
from jax.sharding import PartitionSpec as P

HD = 64


SCALE = 0.125
EPSILON = 1e-06


def normalize(states):
    widened = states.astype(jnp.float32)
    meansq = jnp.mean(widened * widened, axis=-1, keepdims=True)
    inverse = lax.rsqrt(meansq + EPSILON)
    scaled = widened * inverse
    return (scaled, inverse, scaled.astype(jnp.bfloat16))


def project(normed, weights):
    width = weights.shape[1] // 3
    flat = normed.reshape(-1, normed.shape[-1])
    mixed = jnp.dot(flat, weights, preferred_element_type=jnp.float32).astype(jnp.bfloat16)
    mixed = mixed.reshape(normed.shape[:-1] + (3 * width,))
    return (mixed[..., :width], mixed[..., width : 2 * width], mixed[..., 2 * width :])


def attend_back(query, key, value, grads, groups):
    batch, rows, features = query.shape
    heads = features // HD
    own = (
        lax.broadcasted_iota(jnp.int32, (heads, features), 1) // HD
        == lax.broadcasted_iota(jnp.int32, (heads, features), 0)
    )

    def by_head(x):
        return jnp.where(own[None, :, None, :], x[:, None], jnp.zeros((), x.dtype))

    query_heads = by_head(query)
    key_heads = by_head(key)
    grad_heads = by_head(grads)
    scores = (
        jnp.einsum("bhid,bjd->bhij", query_heads, key, preferred_element_type=jnp.float32)
        * SCALE
    )
    header = lax.broadcasted_iota(jnp.int32, (rows, rows), 1) == 0
    visible = (groups[:, :, None] == groups[:, None, :]) | header
    scores = jnp.where(visible[:, None], scores, -1e30)
    peak = jnp.max(scores, axis=-1, keepdims=True)
    expsc = jnp.exp(scores - peak)
    probs = expsc / jnp.sum(expsc, axis=-1, keepdims=True)
    probs_low = probs.astype(jnp.bfloat16)
    value_grad = jnp.einsum(
        "bhij,bhid->bjd", probs_low, grad_heads, preferred_element_type=jnp.float32
    ).astype(jnp.bfloat16)
    prob_grad = jnp.einsum(
        "bhid,bjd->bhij", grad_heads, value, preferred_element_type=jnp.float32
    )
    score_grad = probs * (prob_grad - jnp.sum(probs * prob_grad, axis=-1, keepdims=True))
    score_low = (score_grad * SCALE).astype(jnp.bfloat16)
    query_grad = jnp.einsum(
        "bhij,bhjd->bid", score_low, key_heads, preferred_element_type=jnp.float32
    ).astype(jnp.bfloat16)
    key_grad = jnp.einsum(
        "bhij,bhid->bjd", score_low, query_heads, preferred_element_type=jnp.float32
    ).astype(jnp.bfloat16)
    return (query_grad, key_grad, value_grad)


def finish(scaled, inverse, normed, all_grads, weights):
    flat_norm = normed.reshape(-1, normed.shape[-1])
    flat_grad = all_grads.reshape(-1, all_grads.shape[-1])
    partial_w = lax.dot_general(
        flat_norm, flat_grad, (((0,), (0,)), ((), ())), preferred_element_type=jnp.float32
    )
    normed_grad = lax.dot_general(
        flat_grad, weights, (((1,), (1,)), ((), ())), preferred_element_type=jnp.float32
    )
    normed_grad = normed_grad.reshape(scaled.shape)
    coupling = jnp.mean(normed_grad * scaled, axis=-1, keepdims=True)
    state_grad = (inverse * (normed_grad - scaled * coupling)).astype(jnp.bfloat16)
    return (partial_w, state_grad)


def exchange(blocks, dim, digit, stride, n, wire=jnp.float32):
    mine = lax.dynamic_index_in_dim(blocks, digit, axis=dim, keepdims=False)
    total = mine.astype(jnp.float32)
    n_band = lax.axis_size("band")
    for shift in range(1, n):
        part = lax.dynamic_index_in_dim(blocks, (digit + shift) % n, axis=dim, keepdims=False)
        pairs = []
        for source in range(n_band):
            d = (source // stride) % n
            pairs.append((source, source + (((d + shift) % n) - d) * stride))
        got = lax.ppermute(part.astype(wire), "band", pairs)
        total = total + got.astype(jnp.float32)
    return total


def band_stages(partial_w):
    n_band = lax.axis_size("band")
    d_in, d_out = partial_w.shape
    rows = d_in // n_band
    band = lax.axis_index("band")
    blocks = partial_w.reshape(n_band // 4, 2, 2, rows, d_out)
    blocks = exchange(blocks, 2, band % 2, 1, 2)
    blocks = exchange(blocks, 0, band // 4, 4, n_band // 4, jnp.bfloat16)
    return exchange(blocks, 0, (band // 2) % 2, 2, 2)


def dp_stage(blocks):
    n_dp = lax.axis_size("dp")
    rows, d_out = blocks.shape
    cols = d_out // n_dp
    blocks = blocks.reshape(rows, n_dp, cols).transpose(1, 0, 2)
    blocks = lax.all_to_all(blocks, "dp", 0, 0, tiled=True)
    return blocks.sum(axis=0)


def body(cell_states, head_grads, group_ids, proj_weights):
    width = cell_states.shape[-1]
    states_cols = lax.all_to_all(cell_states, "band", split_axis=2, concat_axis=1, tiled=True)
    tables, rows, cols, _ = states_cols.shape
    states_cols = states_cols.transpose(0, 2, 1, 3).reshape(tables * cols, rows, width)
    grads_by_col = head_grads.transpose(2, 0, 1, 3)
    states_cols, grads_by_col = lax.optimization_barrier((states_cols, grads_by_col))
    grad_cols = lax.all_to_all(grads_by_col, "band", split_axis=0, concat_axis=2, tiled=True)
    grad_cols = grad_cols.transpose(1, 0, 2, 3).reshape(tables * cols, rows, -1)
    groups = group_ids.reshape(tables * cols, rows)
    scaled, inverse, normed = normalize(states_cols)
    query_cols, key_cols, value_cols = project(normed, proj_weights)
    query_grad, key_grad, value_grad = attend_back(
        query_cols, key_cols, value_cols, grad_cols, groups
    )
    all_grads = jnp.concatenate((query_grad, key_grad, value_grad), axis=-1)
    partial_w, input_cols = finish(scaled, inverse, normed, all_grads, proj_weights)
    input_cols = input_cols.reshape(tables, cols, rows, width).transpose(0, 2, 1, 3)
    input_cols, partial_w = lax.optimization_barrier((input_cols, partial_w))
    input_grad = lax.all_to_all(input_cols, "band", split_axis=1, concat_axis=2, tiled=True)
    reduced = band_stages(partial_w)
    reduced, input_grad = lax.optimization_barrier((reduced, input_grad))
    weight_grad = dp_stage(reduced)
    return (input_grad, weight_grad)


def solution(mesh):
    return jax.shard_map(
        body,
        mesh=mesh,
        in_specs=(
            P("dp", "band", None, None),
            P("dp", "band", None, None),
            P("dp", "band", None),
            P(),
        ),
        out_specs=(P("dp", "band", None, None), P("band", "dp")),
        check_vma=False,
    )
```

```python
import jax
import jax.numpy as jnp
from jax import lax
from jax.sharding import PartitionSpec as P

HD = 64


SCALE = 0.125
EPSILON = 1e-06


def normalize(states):
    widened = states.astype(jnp.float32)
    meansq = jnp.mean(widened * widened, axis=-1, keepdims=True)
    inverse = lax.rsqrt(meansq + EPSILON)
    scaled = widened * inverse
    return (scaled, inverse, scaled.astype(jnp.bfloat16))


def project(normed, weights):
    width = weights.shape[1] // 3
    flat = normed.reshape(-1, normed.shape[-1])
    mixed = jnp.dot(flat, weights, preferred_element_type=jnp.float32).astype(jnp.bfloat16)
    mixed = mixed.reshape(normed.shape[:-1] + (3 * width,))
    return (mixed[..., :width], mixed[..., width : 2 * width], mixed[..., 2 * width :])


def attend_back(query, key, value, grads, groups):
    batch, rows, features = query.shape
    heads = features // HD
    own = (
        lax.broadcasted_iota(jnp.int32, (heads, features), 1) // HD
        == lax.broadcasted_iota(jnp.int32, (heads, features), 0)
    )

    def by_head(x):
        return jnp.where(own[None, :, None, :], x[:, None], jnp.zeros((), x.dtype))

    query_heads = by_head(query)
    key_heads = by_head(key)
    grad_heads = by_head(grads)
    scores = (
        jnp.einsum("bhid,bjd->bhij", query_heads, key, preferred_element_type=jnp.float32)
        * SCALE
    )
    header = lax.broadcasted_iota(jnp.int32, (rows, rows), 1) == 0
    visible = (groups[:, :, None] == groups[:, None, :]) | header
    scores = jnp.where(visible[:, None], scores, -1e30)
    peak = jnp.max(scores, axis=-1, keepdims=True)
    expsc = jnp.exp(scores - peak)
    probs = expsc / jnp.sum(expsc, axis=-1, keepdims=True)
    probs_low = probs.astype(jnp.bfloat16)
    value_grad = jnp.einsum(
        "bhij,bhid->bjd", probs_low, grad_heads, preferred_element_type=jnp.float32
    ).astype(jnp.bfloat16)
    prob_grad = jnp.einsum(
        "bhid,bjd->bhij", grad_heads, value, preferred_element_type=jnp.float32
    )
    score_grad = probs * (prob_grad - jnp.sum(probs * prob_grad, axis=-1, keepdims=True))
    score_low = (score_grad * SCALE).astype(jnp.bfloat16)
    query_grad = jnp.einsum(
        "bhij,bhjd->bid", score_low, key_heads, preferred_element_type=jnp.float32
    ).astype(jnp.bfloat16)
    key_grad = jnp.einsum(
        "bhij,bhid->bjd", score_low, query_heads, preferred_element_type=jnp.float32
    ).astype(jnp.bfloat16)
    return (query_grad, key_grad, value_grad)


def finish(scaled, inverse, normed, all_grads, weights):
    flat_norm = normed.reshape(-1, normed.shape[-1])
    flat_grad = all_grads.reshape(-1, all_grads.shape[-1])
    partial_w = lax.dot_general(
        flat_norm, flat_grad, (((0,), (0,)), ((), ())), preferred_element_type=jnp.float32
    )
    normed_grad = lax.dot_general(
        flat_grad, weights, (((1,), (1,)), ((), ())), preferred_element_type=jnp.float32
    )
    normed_grad = normed_grad.reshape(scaled.shape)
    coupling = jnp.mean(normed_grad * scaled, axis=-1, keepdims=True)
    state_grad = (inverse * (normed_grad - scaled * coupling)).astype(jnp.bfloat16)
    return (partial_w, state_grad)


def exchange(blocks, dim, digit, stride, n, wire=jnp.float32):
    mine = lax.dynamic_index_in_dim(blocks, digit, axis=dim, keepdims=False)
    total = mine.astype(jnp.float32)
    n_band = lax.axis_size("band")
    for shift in range(1, n):
        part = lax.dynamic_index_in_dim(blocks, (digit + shift) % n, axis=dim, keepdims=False)
        pairs = []
        for source in range(n_band):
            d = (source // stride) % n
            pairs.append((source, source + (((d + shift) % n) - d) * stride))
        got = lax.ppermute(part.astype(wire), "band", pairs)
        total = total + got.astype(jnp.float32)
    return total


def band_stages(partial_w):
    n_band = lax.axis_size("band")
    d_in, d_out = partial_w.shape
    rows = d_in // n_band
    band = lax.axis_index("band")
    blocks = partial_w.reshape(n_band // 4, 2, 2, rows, d_out)
    blocks = exchange(blocks, 2, band % 2, 1, 2)
    blocks = exchange(blocks, 0, band // 4, 4, n_band // 4, jnp.bfloat16)
    return exchange(blocks, 0, (band // 2) % 2, 2, 2)


def dp_stage(blocks):
    n_dp = lax.axis_size("dp")
    rows, d_out = blocks.shape
    cols = d_out // n_dp
    blocks = blocks.reshape(rows, n_dp, cols).transpose(1, 0, 2)
    blocks = lax.all_to_all(blocks.astype(jnp.bfloat16), "dp", 0, 0, tiled=True)
    return blocks.astype(jnp.float32).sum(axis=0)


def body(cell_states, head_grads, group_ids, proj_weights):
    width = cell_states.shape[-1]
    states_cols = lax.all_to_all(cell_states, "band", split_axis=2, concat_axis=1, tiled=True)
    tables, rows, cols, _ = states_cols.shape
    states_cols = states_cols.transpose(0, 2, 1, 3).reshape(tables * cols, rows, width)
    grads_by_col = head_grads.transpose(2, 0, 1, 3)
    states_cols, grads_by_col = lax.optimization_barrier((states_cols, grads_by_col))
    grad_cols = lax.all_to_all(grads_by_col, "band", split_axis=0, concat_axis=2, tiled=True)
    grad_cols = grad_cols.transpose(1, 0, 2, 3).reshape(tables * cols, rows, -1)
    groups = group_ids.reshape(tables * cols, rows)
    scaled, inverse, normed = normalize(states_cols)
    query_cols, key_cols, value_cols = project(normed, proj_weights)
    query_grad, key_grad, value_grad = attend_back(
        query_cols, key_cols, value_cols, grad_cols, groups
    )
    all_grads = jnp.concatenate((query_grad, key_grad, value_grad), axis=-1)
    partial_w, input_cols = finish(scaled, inverse, normed, all_grads, proj_weights)
    input_cols = input_cols.reshape(tables, cols, rows, width).transpose(0, 2, 1, 3)
    input_cols, partial_w = lax.optimization_barrier((input_cols, partial_w))
    input_grad = lax.all_to_all(input_cols, "band", split_axis=1, concat_axis=2, tiled=True)
    reduced = band_stages(partial_w)
    reduced, input_grad = lax.optimization_barrier((reduced, input_grad))
    weight_grad = dp_stage(reduced)
    return (input_grad, weight_grad)


def solution(mesh):
    return jax.shard_map(
        body,
        mesh=mesh,
        in_specs=(
            P("dp", "band", None, None),
            P("dp", "band", None, None),
            P("dp", "band", None),
            P(),
        ),
        out_specs=(P("dp", "band", None, None), P("band", "dp")),
        check_vma=False,
    )
```

```python
import jax
import jax.numpy as jnp
from jax import lax
from jax.sharding import PartitionSpec as P

HD = 64


SCALE = 0.125
EPSILON = 1e-06


def normalize(states):
    widened = states.astype(jnp.float32)
    meansq = jnp.mean(widened * widened, axis=-1, keepdims=True)
    inverse = lax.rsqrt(meansq + EPSILON)
    scaled = widened * inverse
    return (scaled, inverse, scaled.astype(jnp.bfloat16))


def project(normed, weights):
    width = weights.shape[1] // 3
    flat = normed.reshape(-1, normed.shape[-1])
    mixed = jnp.dot(flat, weights, preferred_element_type=jnp.float32).astype(jnp.bfloat16)
    mixed = mixed.reshape(normed.shape[:-1] + (3 * width,))
    return (mixed[..., :width], mixed[..., width : 2 * width], mixed[..., 2 * width :])


def attend_back(query, key, value, grads, groups):
    batch, rows, features = query.shape
    heads = features // HD
    own = (
        lax.broadcasted_iota(jnp.int32, (heads, features), 1) // HD
        == lax.broadcasted_iota(jnp.int32, (heads, features), 0)
    )

    def by_head(x):
        return jnp.where(own[None, :, None, :], x[:, None], jnp.zeros((), x.dtype))

    query_heads = by_head(query)
    key_heads = by_head(key)
    grad_heads = by_head(grads)
    scores = (
        jnp.einsum("bhid,bjd->bhij", query_heads, key, preferred_element_type=jnp.float32)
        * SCALE
    )
    header = lax.broadcasted_iota(jnp.int32, (rows, rows), 1) == 0
    visible = (groups[:, :, None] == groups[:, None, :]) | header
    scores = jnp.where(visible[:, None], scores, -1e30)
    peak = jnp.max(scores, axis=-1, keepdims=True)
    expsc = jnp.exp(scores - peak)
    probs = expsc / jnp.sum(expsc, axis=-1, keepdims=True)
    probs_low = probs.astype(jnp.bfloat16)
    value_grad = jnp.einsum(
        "bhij,bhid->bjd", probs_low, grad_heads, preferred_element_type=jnp.float32
    ).astype(jnp.bfloat16)
    prob_grad = jnp.einsum(
        "bhid,bjd->bhij", grad_heads, value, preferred_element_type=jnp.float32
    )
    score_grad = probs * (prob_grad - jnp.sum(probs * prob_grad, axis=-1, keepdims=True))
    score_low = (score_grad * SCALE).astype(jnp.bfloat16)
    query_grad = jnp.einsum(
        "bhij,bhjd->bid", score_low, key_heads, preferred_element_type=jnp.float32
    ).astype(jnp.bfloat16)
    key_grad = jnp.einsum(
        "bhij,bhid->bjd", score_low, query_heads, preferred_element_type=jnp.float32
    ).astype(jnp.bfloat16)
    return (query_grad, key_grad, value_grad)


def finish(scaled, inverse, normed, all_grads, weights):
    flat_norm = normed.reshape(-1, normed.shape[-1])
    flat_grad = all_grads.reshape(-1, all_grads.shape[-1])
    partial_w = lax.dot_general(
        flat_norm, flat_grad, (((0,), (0,)), ((), ())), preferred_element_type=jnp.float32
    )
    normed_grad = lax.dot_general(
        flat_grad, weights, (((1,), (1,)), ((), ())), preferred_element_type=jnp.float32
    )
    normed_grad = normed_grad.reshape(scaled.shape)
    coupling = jnp.mean(normed_grad * scaled, axis=-1, keepdims=True)
    state_grad = (inverse * (normed_grad - scaled * coupling)).astype(jnp.bfloat16)
    return (partial_w, state_grad)


def exchange(blocks, dim, digit, stride, n, wire=jnp.float32):
    mine = lax.dynamic_index_in_dim(blocks, digit, axis=dim, keepdims=False)
    total = mine.astype(jnp.float32)
    n_band = lax.axis_size("band")
    for shift in range(1, n):
        part = lax.dynamic_index_in_dim(blocks, (digit + shift) % n, axis=dim, keepdims=False)
        pairs = []
        for source in range(n_band):
            d = (source // stride) % n
            pairs.append((source, source + (((d + shift) % n) - d) * stride))
        got = lax.ppermute(part.astype(wire), "band", pairs)
        total = total + got.astype(jnp.float32)
    return total


def band_stages(partial_w):
    n_band = lax.axis_size("band")
    d_in, d_out = partial_w.shape
    rows = d_in // n_band
    band = lax.axis_index("band")
    blocks = partial_w.reshape(n_band // 4, 2, 2, rows, d_out)
    blocks = exchange(blocks, 2, band % 2, 1, 2)
    return exchange(blocks, 0, band // 4, 4, n_band // 4, jnp.bfloat16)


def dp_stage(blocks):
    n_dp = lax.axis_size("dp")
    halves, rows, d_out = blocks.shape
    cols = d_out // n_dp
    blocks = blocks.reshape(halves, rows, n_dp, cols).transpose(2, 0, 1, 3)
    blocks = lax.all_to_all(blocks.astype(jnp.bfloat16), "dp", 0, 0, tiled=True)
    blocks = blocks.astype(jnp.float32).sum(axis=0)
    band = lax.axis_index("band")
    return exchange(blocks, 0, (band // 2) % 2, 2, 2)


def body(cell_states, head_grads, group_ids, proj_weights):
    width = cell_states.shape[-1]
    states_cols = lax.all_to_all(cell_states, "band", split_axis=2, concat_axis=1, tiled=True)
    tables, rows, cols, _ = states_cols.shape
    states_cols = states_cols.transpose(0, 2, 1, 3).reshape(tables * cols, rows, width)
    grads_by_col = head_grads.transpose(2, 0, 1, 3)
    states_cols, grads_by_col = lax.optimization_barrier((states_cols, grads_by_col))
    grad_cols = lax.all_to_all(grads_by_col, "band", split_axis=0, concat_axis=2, tiled=True)
    grad_cols = grad_cols.transpose(1, 0, 2, 3).reshape(tables * cols, rows, -1)
    groups = group_ids.reshape(tables * cols, rows)
    scaled, inverse, normed = normalize(states_cols)
    query_cols, key_cols, value_cols = project(normed, proj_weights)
    query_grad, key_grad, value_grad = attend_back(
        query_cols, key_cols, value_cols, grad_cols, groups
    )
    all_grads = jnp.concatenate((query_grad, key_grad, value_grad), axis=-1)
    partial_w, input_cols = finish(scaled, inverse, normed, all_grads, proj_weights)
    input_cols = input_cols.reshape(tables, cols, rows, width).transpose(0, 2, 1, 3)
    input_cols, partial_w = lax.optimization_barrier((input_cols, partial_w))
    input_grad = lax.all_to_all(input_cols, "band", split_axis=1, concat_axis=2, tiled=True)
    reduced = band_stages(partial_w)
    reduced, input_grad = lax.optimization_barrier((reduced, input_grad))
    weight_grad = dp_stage(reduced)
    return (input_grad, weight_grad)


def solution(mesh):
    return jax.shard_map(
        body,
        mesh=mesh,
        in_specs=(
            P("dp", "band", None, None),
            P("dp", "band", None, None),
            P("dp", "band", None),
            P(),
        ),
        out_specs=(P("dp", "band", None, None), P("band", "dp")),
        check_vma=False,
    )
```

```python
import jax
import jax.numpy as jnp
from jax import lax
from jax.sharding import PartitionSpec as P

HD = 64


SCALE = 0.125
EPSILON = 1e-06


def normalize(states):
    widened = states.astype(jnp.float32)
    meansq = jnp.mean(widened * widened, axis=-1, keepdims=True)
    inverse = lax.rsqrt(meansq + EPSILON)
    scaled = widened * inverse
    return (scaled, inverse, scaled.astype(jnp.bfloat16))


def project(normed, weights):
    width = weights.shape[1] // 3
    flat = normed.reshape(-1, normed.shape[-1])
    mixed = jnp.dot(flat, weights, preferred_element_type=jnp.float32).astype(jnp.bfloat16)
    mixed = mixed.reshape(normed.shape[:-1] + (3 * width,))
    return (mixed[..., :width], mixed[..., width : 2 * width], mixed[..., 2 * width :])


def attend_back(query, key, value, grads, groups):
    batch, rows, features = query.shape
    heads = features // HD
    own = (
        lax.broadcasted_iota(jnp.int32, (heads, features), 1) // HD
        == lax.broadcasted_iota(jnp.int32, (heads, features), 0)
    )

    def by_head(x):
        return jnp.where(own[None, :, None, :], x[:, None], jnp.zeros((), x.dtype))

    query_heads = by_head(query)
    key_heads = by_head(key)
    value_heads = by_head(value)
    grad_heads = by_head(grads)
    scores = (
        jnp.einsum("bid,bhjd->bihj", query, key_heads, preferred_element_type=jnp.float32)
        * SCALE
    )
    header = lax.broadcasted_iota(jnp.int32, (rows, rows), 1) == 0
    visible = (groups[:, :, None] == groups[:, None, :]) | header
    scores = jnp.where(visible[:, :, None], scores, -1e30)
    peak = jnp.max(scores, axis=-1, keepdims=True)
    expsc = jnp.exp(scores - peak)
    probs = expsc / jnp.sum(expsc, axis=-1, keepdims=True)
    probs_low = probs.astype(jnp.bfloat16)
    value_grad = jnp.einsum(
        "bihj,bhid->bjd", probs_low, grad_heads, preferred_element_type=jnp.float32
    ).astype(jnp.bfloat16)
    prob_grad = jnp.einsum(
        "bid,bhjd->bihj", grads, value_heads, preferred_element_type=jnp.float32
    )
    score_grad = probs * (prob_grad - jnp.sum(probs * prob_grad, axis=-1, keepdims=True))
    score_low = (score_grad * SCALE).astype(jnp.bfloat16)
    query_grad = jnp.einsum(
        "bihj,bhjd->bid", score_low, key_heads, preferred_element_type=jnp.float32
    ).astype(jnp.bfloat16)
    key_grad = jnp.einsum(
        "bihj,bhid->bjd", score_low, query_heads, preferred_element_type=jnp.float32
    ).astype(jnp.bfloat16)
    return (query_grad, key_grad, value_grad)


def finish(scaled, inverse, normed, all_grads, weights):
    flat_norm = normed.reshape(-1, normed.shape[-1])
    flat_grad = all_grads.reshape(-1, all_grads.shape[-1])
    partial_w = lax.dot_general(
        flat_norm, flat_grad, (((0,), (0,)), ((), ())), preferred_element_type=jnp.float32
    )
    normed_grad = lax.dot_general(
        flat_grad, weights, (((1,), (1,)), ((), ())), preferred_element_type=jnp.float32
    )
    normed_grad = normed_grad.reshape(scaled.shape)
    coupling = jnp.mean(normed_grad * scaled, axis=-1, keepdims=True)
    state_grad = (inverse * (normed_grad - scaled * coupling)).astype(jnp.bfloat16)
    return (partial_w, state_grad)


def exchange(blocks, dim, digit, stride, n, wire=jnp.float32):
    mine = lax.dynamic_index_in_dim(blocks, digit, axis=dim, keepdims=False)
    total = mine.astype(jnp.float32)
    n_band = lax.axis_size("band")
    for shift in range(1, n):
        part = lax.dynamic_index_in_dim(blocks, (digit + shift) % n, axis=dim, keepdims=False)
        pairs = []
        for source in range(n_band):
            d = (source // stride) % n
            pairs.append((source, source + (((d + shift) % n) - d) * stride))
        got = lax.ppermute(part.astype(wire), "band", pairs)
        total = total + got.astype(jnp.float32)
    return total


def band_stages(partial_w):
    n_band = lax.axis_size("band")
    d_in, d_out = partial_w.shape
    rows = d_in // n_band
    band = lax.axis_index("band")
    blocks = partial_w.reshape(n_band // 4, 2, 2, rows, d_out)
    blocks = exchange(blocks, 2, band % 2, 1, 2)
    blocks = exchange(blocks, 0, band // 4, 4, n_band // 4, jnp.bfloat16)
    return exchange(blocks, 0, (band // 2) % 2, 2, 2)


def dp_stage(blocks):
    n_dp = lax.axis_size("dp")
    rows, d_out = blocks.shape
    cols = d_out // n_dp
    blocks = blocks.reshape(rows, n_dp, cols).transpose(1, 0, 2)
    blocks = lax.all_to_all(blocks.astype(jnp.bfloat16), "dp", 0, 0, tiled=True)
    return blocks.astype(jnp.float32).sum(axis=0)


def body(cell_states, head_grads, group_ids, proj_weights):
    width = cell_states.shape[-1]
    states_cols = lax.all_to_all(cell_states, "band", split_axis=2, concat_axis=1, tiled=True)
    tables, rows, cols, _ = states_cols.shape
    states_cols = states_cols.transpose(0, 2, 1, 3).reshape(tables * cols, rows, width)
    grads_by_col = head_grads.transpose(2, 0, 1, 3)
    states_cols, grads_by_col = lax.optimization_barrier((states_cols, grads_by_col))
    grad_cols = lax.all_to_all(grads_by_col, "band", split_axis=0, concat_axis=2, tiled=True)
    grad_cols = grad_cols.transpose(1, 0, 2, 3).reshape(tables * cols, rows, -1)
    groups = group_ids.reshape(tables * cols, rows)
    scaled, inverse, normed = normalize(states_cols)
    query_cols, key_cols, value_cols = project(normed, proj_weights)
    query_grad, key_grad, value_grad = attend_back(
        query_cols, key_cols, value_cols, grad_cols, groups
    )
    all_grads = jnp.concatenate((query_grad, key_grad, value_grad), axis=-1)
    partial_w, input_cols = finish(scaled, inverse, normed, all_grads, proj_weights)
    input_cols = input_cols.reshape(tables, cols, rows, width).transpose(0, 2, 1, 3)
    input_cols, partial_w = lax.optimization_barrier((input_cols, partial_w))
    input_grad = lax.all_to_all(input_cols, "band", split_axis=1, concat_axis=2, tiled=True)
    reduced = band_stages(partial_w)
    reduced, input_grad = lax.optimization_barrier((reduced, input_grad))
    weight_grad = dp_stage(reduced)
    return (input_grad, weight_grad)


def solution(mesh):
    return jax.shard_map(
        body,
        mesh=mesh,
        in_specs=(
            P("dp", "band", None, None),
            P("dp", "band", None, None),
            P("dp", "band", None),
            P(),
        ),
        out_specs=(P("dp", "band", None, None), P("band", "dp")),
        check_vma=False,
    )
```

```python
import jax
import jax.numpy as jnp
from jax import lax
from jax.sharding import PartitionSpec as P

HD = 64


SCALE = 0.125
EPSILON = 1e-06


def normalize(states):
    widened = states.astype(jnp.float32)
    meansq = jnp.mean(widened * widened, axis=-1, keepdims=True)
    inverse = lax.rsqrt(meansq + EPSILON)
    scaled = widened * inverse
    return (scaled, inverse, scaled.astype(jnp.bfloat16))


def project(normed, weights):
    width = weights.shape[1] // 3
    flat = normed.reshape(-1, normed.shape[-1])
    mixed = jnp.dot(flat, weights, preferred_element_type=jnp.float32).astype(jnp.bfloat16)
    mixed = mixed.reshape(normed.shape[:-1] + (3 * width,))
    return (mixed[..., :width], mixed[..., width : 2 * width], mixed[..., 2 * width :])


def attend_back(query, key, value, grads, groups):
    batch, rows, features = query.shape
    heads = features // HD
    own = (
        lax.broadcasted_iota(jnp.int32, (heads, features), 1) // HD
        == lax.broadcasted_iota(jnp.int32, (heads, features), 0)
    )

    def by_head(x):
        return jnp.where(own[None, :, None, :], x[:, None], jnp.zeros((), x.dtype))

    query_heads = by_head(query)
    key_heads = by_head(key)
    value_heads = by_head(value)
    grad_heads = by_head(grads)
    scores = (
        jnp.einsum("bid,bhjd->bihj", query, key_heads, preferred_element_type=jnp.float32)
        * SCALE
    )
    header = lax.broadcasted_iota(jnp.int32, (rows, rows), 1) == 0
    visible = (groups[:, :, None] == groups[:, None, :]) | header
    scores = jnp.where(visible[:, :, None], scores, -1e30)
    peak = jnp.max(scores, axis=-1, keepdims=True)
    expsc = jnp.exp(scores - peak)
    probs = expsc / jnp.sum(expsc, axis=-1, keepdims=True)
    probs_low = probs.astype(jnp.bfloat16)
    value_grad = jnp.einsum(
        "bihj,bhid->bjd", probs_low, grad_heads, preferred_element_type=jnp.float32
    ).astype(jnp.bfloat16)
    prob_grad = jnp.einsum(
        "bid,bhjd->bihj", grads, value_heads, preferred_element_type=jnp.float32
    )
    score_grad = probs * (prob_grad - jnp.sum(probs * prob_grad, axis=-1, keepdims=True))
    score_low = (score_grad * SCALE).astype(jnp.bfloat16)
    query_grad = jnp.einsum(
        "bihj,bhjd->bid", score_low, key_heads, preferred_element_type=jnp.float32
    ).astype(jnp.bfloat16)
    key_grad = jnp.einsum(
        "bihj,bhid->bjd", score_low, query_heads, preferred_element_type=jnp.float32
    ).astype(jnp.bfloat16)
    return (query_grad, key_grad, value_grad)


def finish(scaled, inverse, normed, all_grads, weights):
    flat_norm = normed.reshape(-1, normed.shape[-1])
    flat_grad = all_grads.reshape(-1, all_grads.shape[-1])
    partial_w = lax.dot_general(
        flat_norm, flat_grad, (((0,), (0,)), ((), ())), preferred_element_type=jnp.float32
    )
    normed_grad = lax.dot_general(
        flat_grad, weights, (((1,), (1,)), ((), ())), preferred_element_type=jnp.float32
    )
    normed_grad = normed_grad.reshape(scaled.shape)
    coupling = jnp.mean(normed_grad * scaled, axis=-1, keepdims=True)
    state_grad = (inverse * (normed_grad - scaled * coupling)).astype(jnp.bfloat16)
    return (partial_w, state_grad)


def exchange(blocks, dim, digit, stride, n, wire=jnp.float32):
    mine = lax.dynamic_index_in_dim(blocks, digit, axis=dim, keepdims=False)
    total = mine.astype(jnp.float32)
    n_band = lax.axis_size("band")
    for shift in range(1, n):
        part = lax.dynamic_index_in_dim(blocks, (digit + shift) % n, axis=dim, keepdims=False)
        pairs = []
        for source in range(n_band):
            d = (source // stride) % n
            pairs.append((source, source + (((d + shift) % n) - d) * stride))
        got = lax.ppermute(part.astype(wire), "band", pairs)
        total = total + got.astype(jnp.float32)
    return total


def band_stages(partial_w):
    n_band = lax.axis_size("band")
    d_in, d_out = partial_w.shape
    rows = d_in // n_band
    band = lax.axis_index("band")
    blocks = partial_w.reshape(n_band // 4, 2, 2, rows, d_out)
    blocks = exchange(blocks, 2, band % 2, 1, 2)
    blocks = exchange(blocks, 0, band // 4, 4, n_band // 4, jnp.bfloat16)
    return exchange(blocks, 0, (band // 2) % 2, 2, 2)


def dp_stage(blocks):
    n_dp = lax.axis_size("dp")
    rows, d_out = blocks.shape
    cols = d_out // n_dp
    blocks = blocks.reshape(rows, n_dp, cols).transpose(1, 0, 2)
    blocks = lax.all_to_all(blocks.astype(jnp.bfloat16), "dp", 0, 0, tiled=True)
    return blocks.astype(jnp.float32).sum(axis=0)


def body(cell_states, head_grads, group_ids, proj_weights):
    width = cell_states.shape[-1]
    both = jnp.concatenate((cell_states, head_grads), axis=-1).transpose(2, 0, 1, 3)
    both_cols = lax.all_to_all(both, "band", split_axis=0, concat_axis=2, tiled=True)
    cols, tables, rows, _ = both_cols.shape
    both_cols = both_cols.transpose(1, 0, 2, 3).reshape(tables * cols, rows, -1)
    states_cols = both_cols[..., :width]
    grad_cols = both_cols[..., width:]
    groups = group_ids.reshape(tables * cols, rows)
    scaled, inverse, normed = normalize(states_cols)
    query_cols, key_cols, value_cols = project(normed, proj_weights)
    query_grad, key_grad, value_grad = attend_back(
        query_cols, key_cols, value_cols, grad_cols, groups
    )
    all_grads = jnp.concatenate((query_grad, key_grad, value_grad), axis=-1)
    partial_w, input_cols = finish(scaled, inverse, normed, all_grads, proj_weights)
    input_cols = input_cols.reshape(tables, cols, rows, width).transpose(0, 2, 1, 3)
    input_cols, partial_w = lax.optimization_barrier((input_cols, partial_w))
    input_grad = lax.all_to_all(input_cols, "band", split_axis=1, concat_axis=2, tiled=True)
    reduced = band_stages(partial_w)
    reduced, input_grad = lax.optimization_barrier((reduced, input_grad))
    weight_grad = dp_stage(reduced)
    return (input_grad, weight_grad)


def solution(mesh):
    return jax.shard_map(
        body,
        mesh=mesh,
        in_specs=(
            P("dp", "band", None, None),
            P("dp", "band", None, None),
            P("dp", "band", None),
            P(),
        ),
        out_specs=(P("dp", "band", None, None), P("band", "dp")),
        check_vma=False,
    )
```

```python
import jax
import jax.numpy as jnp
from jax import lax
from jax.sharding import PartitionSpec as P

HD = 64


SCALE = 0.125
EPSILON = 1e-06


def normalize(states):
    widened = states.astype(jnp.float32)
    meansq = jnp.mean(widened * widened, axis=-1, keepdims=True)
    inverse = lax.rsqrt(meansq + EPSILON)
    scaled = widened * inverse
    return (scaled, inverse, scaled.astype(jnp.bfloat16))


def project(normed, weights):
    width = weights.shape[1] // 3
    flat = normed.reshape(-1, normed.shape[-1])
    mixed = jnp.dot(flat, weights, preferred_element_type=jnp.float32).astype(jnp.bfloat16)
    mixed = mixed.reshape(normed.shape[:-1] + (3 * width,))
    return (mixed[..., :width], mixed[..., width : 2 * width], mixed[..., 2 * width :])


def attend_back(query, key, value, grads, groups):
    batch, rows, features = query.shape
    heads = features // HD
    own = (
        lax.broadcasted_iota(jnp.int32, (heads, features), 1) // HD
        == lax.broadcasted_iota(jnp.int32, (heads, features), 0)
    )

    def by_head(x):
        return jnp.where(own[None, :, None, :], x[:, None], jnp.zeros((), x.dtype))

    query_heads = by_head(query)
    key_heads = by_head(key)
    value_heads = by_head(value)
    grad_heads = by_head(grads)
    scores = (
        jnp.einsum("bid,bhjd->bihj", query, key_heads, preferred_element_type=jnp.float32)
        * SCALE
    )
    header = lax.broadcasted_iota(jnp.int32, (rows, rows), 1) == 0
    visible = (groups[:, :, None] == groups[:, None, :]) | header
    scores = jnp.where(visible[:, :, None], scores, -1e30)
    peak = jnp.max(scores, axis=-1, keepdims=True)
    expsc = jnp.exp(scores - peak)
    probs = expsc / jnp.sum(expsc, axis=-1, keepdims=True)
    probs_low = probs.astype(jnp.bfloat16)
    value_grad = jnp.einsum(
        "bihj,bhid->bjd", probs_low, grad_heads, preferred_element_type=jnp.float32
    ).astype(jnp.bfloat16)
    prob_grad = jnp.einsum(
        "bid,bhjd->bihj", grads, value_heads, preferred_element_type=jnp.float32
    )
    score_grad = probs * (prob_grad - jnp.sum(probs * prob_grad, axis=-1, keepdims=True))
    score_low = (score_grad * SCALE).astype(jnp.bfloat16)
    query_grad = jnp.einsum(
        "bihj,bhjd->bid", score_low, key_heads, preferred_element_type=jnp.float32
    ).astype(jnp.bfloat16)
    key_grad = jnp.einsum(
        "bihj,bhid->bjd", score_low, query_heads, preferred_element_type=jnp.float32
    ).astype(jnp.bfloat16)
    return (query_grad, key_grad, value_grad)


def finish(scaled, inverse, normed, all_grads, weights):
    flat_norm = normed.reshape(-1, normed.shape[-1])
    flat_grad = all_grads.reshape(-1, all_grads.shape[-1])
    partial_w = lax.dot_general(
        flat_norm, flat_grad, (((0,), (0,)), ((), ())), preferred_element_type=jnp.float32
    )
    normed_grad = lax.dot_general(
        flat_grad, weights, (((1,), (1,)), ((), ())), preferred_element_type=jnp.float32
    )
    normed_grad = normed_grad.reshape(scaled.shape)
    coupling = jnp.mean(normed_grad * scaled, axis=-1, keepdims=True)
    state_grad = (inverse * (normed_grad - scaled * coupling)).astype(jnp.bfloat16)
    return (partial_w, state_grad)


def exchange(blocks, dim, digit, stride, n, wire=jnp.float32):
    mine = lax.dynamic_index_in_dim(blocks, digit, axis=dim, keepdims=False)
    total = mine.astype(jnp.float32)
    n_band = lax.axis_size("band")
    for shift in range(1, n):
        part = lax.dynamic_index_in_dim(blocks, (digit + shift) % n, axis=dim, keepdims=False)
        pairs = []
        for source in range(n_band):
            d = (source // stride) % n
            pairs.append((source, source + (((d + shift) % n) - d) * stride))
        got = lax.ppermute(part.astype(wire), "band", pairs)
        total = total + got.astype(jnp.float32)
    return total


def band_stages(partial_w):
    n_band = lax.axis_size("band")
    d_in, d_out = partial_w.shape
    rows = d_in // n_band
    band = lax.axis_index("band")
    blocks = partial_w.reshape(n_band // 4, 2, 2, rows, d_out)
    blocks = exchange(blocks, 2, band % 2, 1, 2)
    blocks = exchange(blocks, 0, band // 4, 4, n_band // 4, jnp.bfloat16)
    return exchange(blocks, 0, (band // 2) % 2, 2, 2, jnp.bfloat16)


def dp_stage(blocks):
    n_dp = lax.axis_size("dp")
    rows, d_out = blocks.shape
    cols = d_out // n_dp
    blocks = blocks.reshape(rows, n_dp, cols).transpose(1, 0, 2)
    blocks = lax.all_to_all(blocks.astype(jnp.bfloat16), "dp", 0, 0, tiled=True)
    return blocks.astype(jnp.float32).sum(axis=0)


def body(cell_states, head_grads, group_ids, proj_weights):
    width = cell_states.shape[-1]
    states_cols = lax.all_to_all(cell_states, "band", split_axis=2, concat_axis=1, tiled=True)
    tables, rows, cols, _ = states_cols.shape
    states_cols = states_cols.transpose(0, 2, 1, 3).reshape(tables * cols, rows, width)
    grads_by_col = head_grads.transpose(2, 0, 1, 3)
    states_cols, grads_by_col = lax.optimization_barrier((states_cols, grads_by_col))
    grad_cols = lax.all_to_all(grads_by_col, "band", split_axis=0, concat_axis=2, tiled=True)
    grad_cols = grad_cols.transpose(1, 0, 2, 3).reshape(tables * cols, rows, -1)
    groups = group_ids.reshape(tables * cols, rows)
    scaled, inverse, normed = normalize(states_cols)
    query_cols, key_cols, value_cols = project(normed, proj_weights)
    query_grad, key_grad, value_grad = attend_back(
        query_cols, key_cols, value_cols, grad_cols, groups
    )
    all_grads = jnp.concatenate((query_grad, key_grad, value_grad), axis=-1)
    partial_w, input_cols = finish(scaled, inverse, normed, all_grads, proj_weights)
    input_cols = input_cols.reshape(tables, cols, rows, width).transpose(0, 2, 1, 3)
    input_cols, partial_w = lax.optimization_barrier((input_cols, partial_w))
    input_grad = lax.all_to_all(input_cols, "band", split_axis=1, concat_axis=2, tiled=True)
    reduced = band_stages(partial_w)
    reduced, input_grad = lax.optimization_barrier((reduced, input_grad))
    weight_grad = dp_stage(reduced)
    return (input_grad, weight_grad)


def solution(mesh):
    return jax.shard_map(
        body,
        mesh=mesh,
        in_specs=(
            P("dp", "band", None, None),
            P("dp", "band", None, None),
            P("dp", "band", None),
            P(),
        ),
        out_specs=(P("dp", "band", None, None), P("band", "dp")),
        check_vma=False,
    )
```

```python
import jax
import jax.numpy as jnp
from jax import lax
from jax.sharding import PartitionSpec as P

HD = 64


SCALE = 0.125
EPSILON = 1e-06


def normalize(states):
    widened = states.astype(jnp.float32)
    meansq = jnp.mean(widened * widened, axis=-1, keepdims=True)
    inverse = lax.rsqrt(meansq + EPSILON)
    scaled = widened * inverse
    return (scaled, inverse, scaled.astype(jnp.bfloat16))


def project(normed, weights):
    width = weights.shape[1] // 3
    flat = normed.reshape(-1, normed.shape[-1])
    mixed = jnp.dot(flat, weights, preferred_element_type=jnp.float32).astype(jnp.bfloat16)
    mixed = mixed.reshape(normed.shape[:-1] + (3 * width,))
    return (mixed[..., :width], mixed[..., width : 2 * width], mixed[..., 2 * width :])


def attend_back(query, key, value, grads, groups):
    batch, rows, features = query.shape
    heads = features // HD
    own = (
        lax.broadcasted_iota(jnp.int32, (heads, features), 1) // HD
        == lax.broadcasted_iota(jnp.int32, (heads, features), 0)
    )

    def by_head(x):
        return jnp.where(own[None, :, None, :], x[:, None], jnp.zeros((), x.dtype))

    query_heads = by_head(query)
    key_heads = by_head(key)
    value_heads = by_head(value)
    grad_heads = by_head(grads)
    scores = (
        jnp.einsum("bid,bhjd->bihj", query, key_heads, preferred_element_type=jnp.float32)
        * SCALE
    )
    header = lax.broadcasted_iota(jnp.int32, (rows, rows), 1) == 0
    visible = (groups[:, :, None] == groups[:, None, :]) | header
    scores = jnp.where(visible[:, :, None], scores, -1e30)
    peak = jnp.max(scores, axis=-1, keepdims=True)
    expsc = jnp.exp(scores - peak)
    probs = expsc / jnp.sum(expsc, axis=-1, keepdims=True)
    probs_low = probs.astype(jnp.bfloat16)
    value_grad = jnp.einsum(
        "bihj,bhid->bjd", probs_low, grad_heads, preferred_element_type=jnp.float32
    ).astype(jnp.bfloat16)
    prob_grad = jnp.einsum(
        "bid,bhjd->bihj", grads, value_heads, preferred_element_type=jnp.float32
    )
    score_grad = probs * (prob_grad - jnp.sum(probs * prob_grad, axis=-1, keepdims=True))
    score_low = (score_grad * SCALE).astype(jnp.bfloat16)
    query_grad = jnp.einsum(
        "bihj,bhjd->bid", score_low, key_heads, preferred_element_type=jnp.float32
    ).astype(jnp.bfloat16)
    key_grad = jnp.einsum(
        "bihj,bhid->bjd", score_low, query_heads, preferred_element_type=jnp.float32
    ).astype(jnp.bfloat16)
    return (query_grad, key_grad, value_grad)


def finish(scaled, inverse, normed, all_grads, weights):
    flat_norm = normed.reshape(-1, normed.shape[-1])
    flat_grad = all_grads.reshape(-1, all_grads.shape[-1])
    partial_w = lax.dot_general(
        flat_norm, flat_grad, (((0,), (0,)), ((), ())), preferred_element_type=jnp.float32
    )
    normed_grad = lax.dot_general(
        flat_grad, weights, (((1,), (1,)), ((), ())), preferred_element_type=jnp.float32
    )
    normed_grad = normed_grad.reshape(scaled.shape)
    coupling = jnp.mean(normed_grad * scaled, axis=-1, keepdims=True)
    state_grad = (inverse * (normed_grad - scaled * coupling)).astype(jnp.bfloat16)
    return (partial_w, state_grad)


def exchange(blocks, dim, digit, stride, n, wire=jnp.float32):
    mine = lax.dynamic_index_in_dim(blocks, digit, axis=dim, keepdims=False)
    total = mine.astype(jnp.float32)
    n_band = lax.axis_size("band")
    for shift in range(1, n):
        part = lax.dynamic_index_in_dim(blocks, (digit + shift) % n, axis=dim, keepdims=False)
        pairs = []
        for source in range(n_band):
            d = (source // stride) % n
            pairs.append((source, source + (((d + shift) % n) - d) * stride))
        got = lax.ppermute(part.astype(wire), "band", pairs)
        total = total + got.astype(jnp.float32)
    return total


def band_stages(partial_w):
    n_band = lax.axis_size("band")
    d_in, d_out = partial_w.shape
    rows = d_in // n_band
    band = lax.axis_index("band")
    blocks = partial_w.reshape(n_band // 4, 2, 2, rows, d_out)
    blocks = exchange(blocks, 2, band % 2, 1, 2)
    blocks = exchange(blocks, 0, band // 4, 4, n_band // 4, jnp.bfloat16)
    return exchange(blocks, 0, (band // 2) % 2, 2, 2, jnp.bfloat16)


def dp_stage(blocks):
    n_dp = lax.axis_size("dp")
    rows, d_out = blocks.shape
    cols = d_out // n_dp
    blocks = blocks.reshape(rows, n_dp, cols).transpose(1, 0, 2)
    blocks = lax.all_to_all(blocks.astype(jnp.bfloat16), "dp", 0, 0, tiled=True)
    return blocks.astype(jnp.float32).sum(axis=0)


def body(cell_states, head_grads, group_ids, proj_weights):
    width = cell_states.shape[-1]
    states_cols = lax.all_to_all(cell_states, "band", split_axis=2, concat_axis=1, tiled=True)
    tables, rows, cols, _ = states_cols.shape
    states_cols = states_cols.transpose(0, 2, 1, 3).reshape(tables * cols, rows, width)
    grads_by_col = head_grads.transpose(2, 0, 1, 3)
    states_cols, grads_by_col = lax.optimization_barrier((states_cols, grads_by_col))
    grad_cols = lax.all_to_all(grads_by_col, "band", split_axis=0, concat_axis=2, tiled=True)
    grad_cols = grad_cols.transpose(1, 0, 2, 3).reshape(tables * cols, rows, -1)
    groups = group_ids.reshape(tables * cols, rows)
    scaled, inverse, normed = normalize(states_cols)
    query_cols, key_cols, value_cols = project(normed, proj_weights)
    query_grad, key_grad, value_grad = attend_back(
        query_cols, key_cols, value_cols, grad_cols, groups
    )
    all_grads = jnp.concatenate((query_grad, key_grad, value_grad), axis=-1)
    partial_w, input_cols = finish(scaled, inverse, normed, all_grads, proj_weights)
    input_cols = input_cols.reshape(tables, cols, rows, width).transpose(0, 2, 1, 3)
    input_grad = lax.all_to_all(input_cols, "band", split_axis=1, concat_axis=2, tiled=True)
    reduced = band_stages(partial_w)
    reduced, input_grad = lax.optimization_barrier((reduced, input_grad))
    weight_grad = dp_stage(reduced)
    return (input_grad, weight_grad)


def solution(mesh):
    return jax.shard_map(
        body,
        mesh=mesh,
        in_specs=(
            P("dp", "band", None, None),
            P("dp", "band", None, None),
            P("dp", "band", None),
            P(),
        ),
        out_specs=(P("dp", "band", None, None), P("band", "dp")),
        check_vma=False,
    )
```

```python
import jax
import jax.numpy as jnp
from jax import lax
from jax.sharding import PartitionSpec as P

HD = 64


SCALE = 0.125
EPSILON = 1e-06


def normalize(states):
    widened = states.astype(jnp.float32)
    meansq = jnp.mean(widened * widened, axis=-1, keepdims=True)
    inverse = lax.rsqrt(meansq + EPSILON)
    scaled = widened * inverse
    return (scaled, inverse, scaled.astype(jnp.bfloat16))


def project(normed, weights):
    width = weights.shape[1] // 3
    flat = normed.reshape(-1, normed.shape[-1])
    mixed = jnp.dot(flat, weights, preferred_element_type=jnp.float32).astype(jnp.bfloat16)
    mixed = mixed.reshape(normed.shape[:-1] + (3 * width,))
    return (mixed[..., :width], mixed[..., width : 2 * width], mixed[..., 2 * width :])


def attend_back(query, key, value, grads, groups):
    batch, rows, features = query.shape
    heads = features // HD
    own = (
        lax.broadcasted_iota(jnp.int32, (heads, features), 1) // HD
        == lax.broadcasted_iota(jnp.int32, (heads, features), 0)
    )

    def by_head(x):
        return jnp.where(own[None, :, None, :], x[:, None], jnp.zeros((), x.dtype))

    query_heads = by_head(query)
    key_heads = by_head(key)
    value_heads = by_head(value)
    grad_heads = by_head(grads)
    scores = (
        jnp.einsum("bid,bhjd->bihj", query, key_heads, preferred_element_type=jnp.float32)
        * SCALE
    )
    header = lax.broadcasted_iota(jnp.int32, (rows, rows), 1) == 0
    visible = (groups[:, :, None] == groups[:, None, :]) | header
    scores = jnp.where(visible[:, :, None], scores, -1e30)
    peak = jnp.max(scores, axis=-1, keepdims=True)
    expsc = jnp.exp(scores - peak)
    probs = expsc / jnp.sum(expsc, axis=-1, keepdims=True)
    probs_low = probs.astype(jnp.bfloat16)
    value_grad = jnp.einsum(
        "bihj,bhid->bjd", probs_low, grad_heads, preferred_element_type=jnp.float32
    ).astype(jnp.bfloat16)
    prob_grad = jnp.einsum(
        "bid,bhjd->bihj", grads, value_heads, preferred_element_type=jnp.float32
    )
    score_grad = probs * (prob_grad - jnp.sum(probs * prob_grad, axis=-1, keepdims=True))
    score_low = (score_grad * SCALE).astype(jnp.bfloat16)
    query_grad = jnp.einsum(
        "bihj,bhjd->bid", score_low, key_heads, preferred_element_type=jnp.float32
    ).astype(jnp.bfloat16)
    key_grad = jnp.einsum(
        "bihj,bhid->bjd", score_low, query_heads, preferred_element_type=jnp.float32
    ).astype(jnp.bfloat16)
    return (query_grad, key_grad, value_grad)


def finish(scaled, inverse, normed, all_grads, weights):
    flat_norm = normed.reshape(-1, normed.shape[-1])
    flat_grad = all_grads.reshape(-1, all_grads.shape[-1])
    partial_w = lax.dot_general(
        flat_norm, flat_grad, (((0,), (0,)), ((), ())), preferred_element_type=jnp.float32
    )
    normed_grad = lax.dot_general(
        flat_grad, weights, (((1,), (1,)), ((), ())), preferred_element_type=jnp.float32
    )
    normed_grad = normed_grad.reshape(scaled.shape)
    coupling = jnp.mean(normed_grad * scaled, axis=-1, keepdims=True)
    state_grad = (inverse * (normed_grad - scaled * coupling)).astype(jnp.bfloat16)
    return (partial_w, state_grad)


def exchange(blocks, dim, digit, stride, n, wire=jnp.float32):
    mine = lax.dynamic_index_in_dim(blocks, digit, axis=dim, keepdims=False)
    total = mine.astype(jnp.float32)
    n_band = lax.axis_size("band")
    for shift in range(1, n):
        part = lax.dynamic_index_in_dim(blocks, (digit + shift) % n, axis=dim, keepdims=False)
        pairs = []
        for source in range(n_band):
            d = (source // stride) % n
            pairs.append((source, source + (((d + shift) % n) - d) * stride))
        got = lax.ppermute(part.astype(wire), "band", pairs)
        total = total + got.astype(jnp.float32)
    return total


def band_stages(partial_w):
    n_band = lax.axis_size("band")
    d_in, d_out = partial_w.shape
    rows = d_in // n_band
    band = lax.axis_index("band")
    blocks = partial_w.reshape(n_band // 4, 2, 2, rows, d_out)
    blocks = exchange(blocks, 2, band % 2, 1, 2)
    blocks = exchange(blocks, 0, band // 4, 4, n_band // 4, jnp.bfloat16)
    return exchange(blocks, 0, (band // 2) % 2, 2, 2, jnp.bfloat16)


def dp_stage(blocks):
    n_dp = lax.axis_size("dp")
    rows, d_out = blocks.shape
    cols = d_out // n_dp
    blocks = blocks.reshape(rows, n_dp, cols).transpose(1, 0, 2).reshape(n_dp, rows * cols)
    lanes = -(-rows * cols // 128) * 128
    blocks = jnp.pad(blocks, ((0, 0), (0, lanes - rows * cols))).reshape(n_dp, lanes // 128, 128)
    blocks = lax.all_to_all(blocks.astype(jnp.bfloat16), "dp", 0, 0, tiled=True)
    total = blocks.astype(jnp.float32).sum(axis=0).reshape(lanes)
    return total[: rows * cols].reshape(rows, cols)


def body(cell_states, head_grads, group_ids, proj_weights):
    width = cell_states.shape[-1]
    states_cols = lax.all_to_all(cell_states, "band", split_axis=2, concat_axis=1, tiled=True)
    tables, rows, cols, _ = states_cols.shape
    states_cols = states_cols.transpose(0, 2, 1, 3).reshape(tables * cols, rows, width)
    grads_by_col = head_grads.transpose(2, 0, 1, 3)
    states_cols, grads_by_col = lax.optimization_barrier((states_cols, grads_by_col))
    grad_cols = lax.all_to_all(grads_by_col, "band", split_axis=0, concat_axis=2, tiled=True)
    grad_cols = grad_cols.transpose(1, 0, 2, 3).reshape(tables * cols, rows, -1)
    groups = group_ids.reshape(tables * cols, rows)
    scaled, inverse, normed = normalize(states_cols)
    query_cols, key_cols, value_cols = project(normed, proj_weights)
    query_grad, key_grad, value_grad = attend_back(
        query_cols, key_cols, value_cols, grad_cols, groups
    )
    all_grads = jnp.concatenate((query_grad, key_grad, value_grad), axis=-1)
    partial_w, input_cols = finish(scaled, inverse, normed, all_grads, proj_weights)
    input_cols = input_cols.reshape(tables, cols, rows, width).transpose(0, 2, 1, 3)
    input_cols, partial_w = lax.optimization_barrier((input_cols, partial_w))
    input_grad = lax.all_to_all(input_cols, "band", split_axis=1, concat_axis=2, tiled=True)
    reduced = band_stages(partial_w)
    reduced, input_grad = lax.optimization_barrier((reduced, input_grad))
    weight_grad = dp_stage(reduced)
    return (input_grad, weight_grad)


def solution(mesh):
    return jax.shard_map(
        body,
        mesh=mesh,
        in_specs=(
            P("dp", "band", None, None),
            P("dp", "band", None, None),
            P("dp", "band", None),
            P(),
        ),
        out_specs=(P("dp", "band", None, None), P("band", "dp")),
        check_vma=False,
    )
```

```python
import jax
import jax.numpy as jnp
from jax import lax
from jax.sharding import PartitionSpec as P

HD = 64


SCALE = 0.125
EPSILON = 1e-06


def normalize(states):
    widened = states.astype(jnp.float32)
    meansq = jnp.mean(widened * widened, axis=-1, keepdims=True)
    inverse = lax.rsqrt(meansq + EPSILON)
    scaled = widened * inverse
    return (scaled, inverse, scaled.astype(jnp.bfloat16))


def project(normed, weights):
    width = weights.shape[1] // 3
    flat = normed.reshape(-1, normed.shape[-1])
    mixed = jnp.dot(flat, weights, preferred_element_type=jnp.float32).astype(jnp.bfloat16)
    mixed = mixed.reshape(normed.shape[:-1] + (3 * width,))
    return (mixed[..., :width], mixed[..., width : 2 * width], mixed[..., 2 * width :])


def attend_back(query, key, value, grads, groups):
    batch, rows, features = query.shape
    heads = features // HD
    own = (
        lax.broadcasted_iota(jnp.int32, (heads, features), 1) // HD
        == lax.broadcasted_iota(jnp.int32, (heads, features), 0)
    )

    def by_head(x):
        return jnp.where(own[None, :, None, :], x[:, None], jnp.zeros((), x.dtype))

    query_heads = by_head(query)
    key_heads = by_head(key)
    value_heads = by_head(value)
    grad_heads = by_head(grads)
    scores = (
        jnp.einsum("bid,bhjd->bihj", query, key_heads, preferred_element_type=jnp.float32)
        * SCALE
    )
    header = lax.broadcasted_iota(jnp.int32, (rows, rows), 1) == 0
    visible = (groups[:, :, None] == groups[:, None, :]) | header
    scores = jnp.where(visible[:, :, None], scores, -1e30)
    peak = jnp.max(scores, axis=-1, keepdims=True)
    expsc = jnp.exp(scores - peak)
    probs = expsc / jnp.sum(expsc, axis=-1, keepdims=True)
    probs_low = probs.astype(jnp.bfloat16)
    value_grad = jnp.einsum(
        "bihj,bhid->bjd", probs_low, grad_heads, preferred_element_type=jnp.float32
    ).astype(jnp.bfloat16)
    prob_grad = jnp.einsum(
        "bid,bhjd->bihj", grads, value_heads, preferred_element_type=jnp.float32
    )
    score_grad = probs * (prob_grad - jnp.sum(probs * prob_grad, axis=-1, keepdims=True))
    score_low = (score_grad * SCALE).astype(jnp.bfloat16)
    query_grad = jnp.einsum(
        "bihj,bhjd->bid", score_low, key_heads, preferred_element_type=jnp.float32
    ).astype(jnp.bfloat16)
    key_grad = jnp.einsum(
        "bihj,bhid->bjd", score_low, query_heads, preferred_element_type=jnp.float32
    ).astype(jnp.bfloat16)
    return (query_grad, key_grad, value_grad)


def finish(scaled, inverse, normed, all_grads, weights):
    flat_norm = normed.reshape(-1, normed.shape[-1])
    flat_grad = all_grads.reshape(-1, all_grads.shape[-1])
    partial_w = lax.dot_general(
        flat_norm, flat_grad, (((0,), (0,)), ((), ())), preferred_element_type=jnp.float32
    )
    normed_grad = lax.dot_general(
        flat_grad, weights, (((1,), (1,)), ((), ())), preferred_element_type=jnp.float32
    )
    normed_grad = normed_grad.reshape(scaled.shape)
    coupling = jnp.mean(normed_grad * scaled, axis=-1, keepdims=True)
    state_grad = (inverse * (normed_grad - scaled * coupling)).astype(jnp.bfloat16)
    return (partial_w, state_grad)


def exchange(blocks, dim, digit, stride, n, wire=jnp.float32):
    mine = lax.dynamic_index_in_dim(blocks, digit, axis=dim, keepdims=False)
    total = mine.astype(jnp.float32)
    n_band = lax.axis_size("band")
    for shift in sorted(range(1, n), key=lambda k: -min(k, n - k)):
        part = lax.dynamic_index_in_dim(blocks, (digit + shift) % n, axis=dim, keepdims=False)
        pairs = []
        for source in range(n_band):
            d = (source // stride) % n
            pairs.append((source, source + (((d + shift) % n) - d) * stride))
        got = lax.ppermute(part.astype(wire), "band", pairs)
        total = total + got.astype(jnp.float32)
    return total


def band_stages(partial_w):
    n_band = lax.axis_size("band")
    d_in, d_out = partial_w.shape
    rows = d_in // n_band
    band = lax.axis_index("band")
    blocks = partial_w.reshape(n_band // 4, 2, 2, rows, d_out)
    blocks = exchange(blocks, 2, band % 2, 1, 2)
    blocks = exchange(blocks, 0, band // 4, 4, n_band // 4, jnp.bfloat16)
    return exchange(blocks, 0, (band // 2) % 2, 2, 2, jnp.bfloat16)


def dp_stage(blocks):
    n_dp = lax.axis_size("dp")
    rows, d_out = blocks.shape
    cols = d_out // n_dp
    blocks = blocks.reshape(rows, n_dp, cols).transpose(1, 0, 2).reshape(n_dp, rows * cols)
    lanes = -(-rows * cols // 128) * 128
    blocks = jnp.pad(blocks, ((0, 0), (0, lanes - rows * cols))).reshape(n_dp, lanes // 128, 128)
    blocks = lax.all_to_all(blocks.astype(jnp.bfloat16), "dp", 0, 0, tiled=True)
    total = blocks.astype(jnp.float32).sum(axis=0).reshape(lanes)
    return total[: rows * cols].reshape(rows, cols)


def body(cell_states, head_grads, group_ids, proj_weights):
    width = cell_states.shape[-1]
    states_cols = lax.all_to_all(cell_states, "band", split_axis=2, concat_axis=1, tiled=True)
    tables, rows, cols, _ = states_cols.shape
    states_cols = states_cols.transpose(0, 2, 1, 3).reshape(tables * cols, rows, width)
    grads_by_col = head_grads.transpose(2, 0, 1, 3)
    states_cols, grads_by_col = lax.optimization_barrier((states_cols, grads_by_col))
    grad_cols = lax.all_to_all(grads_by_col, "band", split_axis=0, concat_axis=2, tiled=True)
    grad_cols = grad_cols.transpose(1, 0, 2, 3).reshape(tables * cols, rows, -1)
    groups = group_ids.reshape(tables * cols, rows)
    scaled, inverse, normed = normalize(states_cols)
    query_cols, key_cols, value_cols = project(normed, proj_weights)
    query_grad, key_grad, value_grad = attend_back(
        query_cols, key_cols, value_cols, grad_cols, groups
    )
    all_grads = jnp.concatenate((query_grad, key_grad, value_grad), axis=-1)
    partial_w, input_cols = finish(scaled, inverse, normed, all_grads, proj_weights)
    input_cols = input_cols.reshape(tables, cols, rows, width).transpose(0, 2, 1, 3)
    input_cols, partial_w = lax.optimization_barrier((input_cols, partial_w))
    input_grad = lax.all_to_all(input_cols, "band", split_axis=1, concat_axis=2, tiled=True)
    reduced = band_stages(partial_w)
    reduced, input_grad = lax.optimization_barrier((reduced, input_grad))
    weight_grad = dp_stage(reduced)
    return (input_grad, weight_grad)


def solution(mesh):
    return jax.shard_map(
        body,
        mesh=mesh,
        in_specs=(
            P("dp", "band", None, None),
            P("dp", "band", None, None),
            P("dp", "band", None),
            P(),
        ),
        out_specs=(P("dp", "band", None, None), P("band", "dp")),
        check_vma=False,
    )
```

```python
import jax
import jax.numpy as jnp
from jax import lax
from jax.sharding import PartitionSpec as P

HD = 64


SCALE = 0.125
EPSILON = 1e-06


def normalize(states):
    widened = states.astype(jnp.float32)
    meansq = jnp.mean(widened * widened, axis=-1, keepdims=True)
    inverse = lax.rsqrt(meansq + EPSILON)
    scaled = widened * inverse
    return (scaled, inverse, scaled.astype(jnp.bfloat16))


def project(normed, weights):
    width = weights.shape[1] // 3
    flat = normed.reshape(-1, normed.shape[-1])
    mixed = jnp.dot(flat, weights, preferred_element_type=jnp.float32).astype(jnp.bfloat16)
    mixed = mixed.reshape(normed.shape[:-1] + (3 * width,))
    return (mixed[..., :width], mixed[..., width : 2 * width], mixed[..., 2 * width :])


def attend_back(query, key, value, grads, groups):
    batch, rows, features = query.shape
    heads = features // HD
    own = (
        lax.broadcasted_iota(jnp.int32, (heads, features), 1) // HD
        == lax.broadcasted_iota(jnp.int32, (heads, features), 0)
    )

    def by_head(x):
        return jnp.where(own[None, :, None, :], x[:, None], jnp.zeros((), x.dtype))

    query_heads = by_head(query)
    key_heads = by_head(key)
    value_heads = by_head(value)
    grad_heads = by_head(grads)
    scores = (
        jnp.einsum("bid,bhjd->bihj", query, key_heads, preferred_element_type=jnp.float32)
        * SCALE
    )
    header = lax.broadcasted_iota(jnp.int32, (rows, rows), 1) == 0
    visible = (groups[:, :, None] == groups[:, None, :]) | header
    scores = jnp.where(visible[:, :, None], scores, -1e30)
    peak = jnp.max(scores, axis=-1, keepdims=True)
    expsc = jnp.exp(scores - peak)
    probs = expsc / jnp.sum(expsc, axis=-1, keepdims=True)
    probs_low = probs.astype(jnp.bfloat16)
    value_grad = jnp.einsum(
        "bihj,bhid->bjd", probs_low, grad_heads, preferred_element_type=jnp.float32
    ).astype(jnp.bfloat16)
    prob_grad = jnp.einsum(
        "bid,bhjd->bihj", grads, value_heads, preferred_element_type=jnp.float32
    )
    score_grad = probs * (prob_grad - jnp.sum(probs * prob_grad, axis=-1, keepdims=True))
    score_low = (score_grad * SCALE).astype(jnp.bfloat16)
    query_grad = jnp.einsum(
        "bihj,bhjd->bid", score_low, key_heads, preferred_element_type=jnp.float32
    ).astype(jnp.bfloat16)
    key_grad = jnp.einsum(
        "bihj,bhid->bjd", score_low, query_heads, preferred_element_type=jnp.float32
    ).astype(jnp.bfloat16)
    return (query_grad, key_grad, value_grad)


def finish(scaled, inverse, normed, all_grads, weights):
    flat_norm = normed.reshape(-1, normed.shape[-1])
    flat_grad = all_grads.reshape(-1, all_grads.shape[-1])
    partial_w = lax.dot_general(
        flat_norm, flat_grad, (((0,), (0,)), ((), ())), preferred_element_type=jnp.float32
    )
    normed_grad = lax.dot_general(
        flat_grad, weights, (((1,), (1,)), ((), ())), preferred_element_type=jnp.float32
    )
    normed_grad = normed_grad.reshape(scaled.shape)
    coupling = jnp.mean(normed_grad * scaled, axis=-1, keepdims=True)
    state_grad = (inverse * (normed_grad - scaled * coupling)).astype(jnp.bfloat16)
    return (partial_w, state_grad)


def exchange(blocks, dim, digit, stride, n, wire=jnp.float32):
    mine = lax.dynamic_index_in_dim(blocks, digit, axis=dim, keepdims=False)
    total = mine.astype(jnp.float32)
    n_band = lax.axis_size("band")
    for shift in sorted(range(1, n), key=lambda k: -min(k, n - k)):
        part = lax.dynamic_index_in_dim(blocks, (digit + shift) % n, axis=dim, keepdims=False)
        pairs = []
        for source in range(n_band):
            d = (source // stride) % n
            pairs.append((source, source + (((d + shift) % n) - d) * stride))
        got = lax.ppermute(part.astype(wire), "band", pairs)
        total = total + got.astype(jnp.float32)
    return total


def band_stages(partial_w):
    n_band = lax.axis_size("band")
    d_in, d_out = partial_w.shape
    rows = d_in // n_band
    band = lax.axis_index("band")
    blocks = partial_w.reshape(n_band // 4, 2, 2, rows, d_out)
    blocks = exchange(blocks, 2, band % 2, 1, 2, jnp.bfloat16)
    blocks = exchange(blocks, 0, band // 4, 4, n_band // 4, jnp.bfloat16)
    return exchange(blocks, 0, (band // 2) % 2, 2, 2, jnp.bfloat16)


def dp_stage(blocks):
    n_dp = lax.axis_size("dp")
    rows, d_out = blocks.shape
    cols = d_out // n_dp
    blocks = blocks.reshape(rows, n_dp, cols).transpose(1, 0, 2).reshape(n_dp, rows * cols)
    lanes = -(-rows * cols // 128) * 128
    blocks = jnp.pad(blocks, ((0, 0), (0, lanes - rows * cols))).reshape(n_dp, lanes // 128, 128)
    blocks = lax.all_to_all(blocks.astype(jnp.bfloat16), "dp", 0, 0, tiled=True)
    total = blocks.astype(jnp.float32).sum(axis=0).reshape(lanes)
    return total[: rows * cols].reshape(rows, cols)


def body(cell_states, head_grads, group_ids, proj_weights):
    width = cell_states.shape[-1]
    states_cols = lax.all_to_all(cell_states, "band", split_axis=2, concat_axis=1, tiled=True)
    tables, rows, cols, _ = states_cols.shape
    states_cols = states_cols.transpose(0, 2, 1, 3).reshape(tables * cols, rows, width)
    grads_by_col = head_grads.transpose(2, 0, 1, 3)
    states_cols, grads_by_col = lax.optimization_barrier((states_cols, grads_by_col))
    grad_cols = lax.all_to_all(grads_by_col, "band", split_axis=0, concat_axis=2, tiled=True)
    grad_cols = grad_cols.transpose(1, 0, 2, 3).reshape(tables * cols, rows, -1)
    groups = group_ids.reshape(tables * cols, rows)
    scaled, inverse, normed = normalize(states_cols)
    query_cols, key_cols, value_cols = project(normed, proj_weights)
    query_grad, key_grad, value_grad = attend_back(
        query_cols, key_cols, value_cols, grad_cols, groups
    )
    all_grads = jnp.concatenate((query_grad, key_grad, value_grad), axis=-1)
    partial_w, input_cols = finish(scaled, inverse, normed, all_grads, proj_weights)
    input_cols = input_cols.reshape(tables, cols, rows, width).transpose(0, 2, 1, 3)
    input_cols, partial_w = lax.optimization_barrier((input_cols, partial_w))
    input_grad = lax.all_to_all(input_cols, "band", split_axis=1, concat_axis=2, tiled=True)
    reduced = band_stages(partial_w)
    reduced, input_grad = lax.optimization_barrier((reduced, input_grad))
    weight_grad = dp_stage(reduced)
    return (input_grad, weight_grad)


def solution(mesh):
    return jax.shard_map(
        body,
        mesh=mesh,
        in_specs=(
            P("dp", "band", None, None),
            P("dp", "band", None, None),
            P("dp", "band", None),
            P(),
        ),
        out_specs=(P("dp", "band", None, None), P("band", "dp")),
        check_vma=False,
    )
```
